32 devices in a mesh: grp: 2 (over x), ep: 16 (over z, y, core).
Axes of the slice: x: 2, y: 2, z: 4, core: 2. Of those that a mesh axis runs over, the one named last changes fastest.
Arguments:
- tokens: bfloat16 [2048, 7168], P(('grp', 'ep')), parts along dimension 0, may hold values from -6 to 6
- parents: int32 [2048], P(('grp', 'ep')), parts along dimension 0, may hold values from -1 to 62, as said below
- expert_ids: int32 [2048, 1], P(('grp', 'ep')), parts along dimension 0, may hold values from 0 to 1; in each aligned block of 64 rows (0 to 63, 64 to 127, ...) at most 40 rows name the same one
- route_weights: float32 [2048, 1], P(('grp', 'ep')), parts along dimension 0, may hold values from 0.2 to 2
- w_gate: bfloat16 [16, 7168, 256], P('ep'), may hold values from -0.0625 to 0.0625
- w_up: bfloat16 [16, 7168, 256], P('ep'), may hold values from -0.0625 to 0.0625
- w_down: bfloat16 [16, 256, 7168], P('ep'), may hold values from -0.125 to 0.125
Outputs:
- expert_out: bfloat16 [2048, 7168], P(('grp', 'ep')), parts along dimension 0
The draws below stay inside these ranges and needn't reach their ends.
There are 2 independent parts, one for each index of `grp`. The reference program is written for one: setup_inputs(seed, part) draws one part's arguments, and reference() takes and returns one part's arrays. A program takes and returns all parts, laid end to end along the dimension named above; an argument that names none is the same for every part. Nothing has to cross between parts.
Inputs may be any that keep to these rules, and one draw needn't show every extreme that they name: `parents`: rows 64 * r to 64 * r + 63 form request r. Its first node is the root with parent -1; node n of a request has a parent below n, given as its index within the request. The last node of the last request has parent 64 - 2. `expert_ids`: each row names 1 different experts; among the rows of one device no expert is named more than 40 times, and in every draw some device names some expert exactly 40 times.
All inputs are finite; a program needn't handle non-finite values.
Results may differ from the reference program's by a relative error of at most 0.0072.
Values may be sent and summed in bfloat16 or wider, within the bound.
No kernel may reach another device: no remote copies, remote signals or barrier semaphores. Data moves between devices by JAX's collectives and lax.ppermute only.
A program may use at most 128 MiB of HBM per device.

```python
import math
import jax
import jax.numpy as jnp
import numpy as np
from jax import lax

D = 7168
FF = 2048
SLICES = 8
TOP = 1
TOK_DEV = 64
EXPERTS = 2
FF_DEV = 256
CAP = 40
TOKENS = 1024
N_EP = 16


def draw_parents(key, part):
    rows = jnp.arange(TOKENS, dtype=jnp.int32)
    nodes = rows % TOK_DEV
    picked = jax.random.randint(jax.random.fold_in(key, 7), (TOKENS,), 0, jnp.maximum(nodes, 1))
    picked = jnp.where((rows == TOKENS - 1) & (nodes > 0), TOK_DEV - 2, picked)
    return jnp.where(nodes == 0, -1, picked).astype(jnp.int32)


def block_levels(rng, dims, split, least, top_value):
    factor_of, own = 1.0, jax.random.fold_in(rng, 6)
    for axis_at, blocks in split:
        steps = jnp.exp(jax.random.uniform(jax.random.fold_in(own, axis_at), (blocks,), jnp.float32, least / len(split), top_value / len(split)))
        factor_of = factor_of * jnp.repeat(steps, dims[axis_at] // blocks).reshape([-1 if axis == axis_at else 1 for axis in range(len(dims))])
    return factor_of


def assign_block(own_key, own, number, rows, number_of, top, reach, slope):
    order = jax.random.permutation(own_key, number_of)
    crowded, ordinary = shares(number_of, rows * top, reach, slope, True), shares(number_of, rows * top, reach, slope, False)
    places = jnp.arange(number_of)

    def named(lengths, offset_by):
        used = int((lengths > 0).sum())
        fixed = max(1, used // 4)
        moved = fixed + (places - fixed + offset_by * (used - fixed)) % max(1, number_of - fixed)
        return jnp.zeros((number_of,), jnp.int32).at[order[jnp.where(places < fixed, places, moved)]].set(jnp.asarray(lengths, jnp.int32))

    lengths = jnp.where(number % 4 == 0, named(crowded, number // 4), named(ordinary, number - number // 4 - 1))
    mixed = jax.random.permutation(jax.random.fold_in(own, 3), number_of)
    giver, sink = mixed[0:number_of // 2 * 2:2], mixed[1:number_of // 2 * 2:2]
    slack = jnp.minimum(lengths[giver] - 1, reach - lengths[sink]) // 2
    slack = jnp.where((giver == order[0]) | (sink == order[0]) | (lengths[sink] == 0), 0, jnp.maximum(slack, 0))
    moved = jax.random.randint(jax.random.fold_in(own, 4), (number_of // 2,), 0, 1 << 20) % (slack + 1)
    lengths = lengths.at[giver].add(-moved).at[sink].add(moved)
    members = jnp.searchsorted(jnp.cumsum(lengths), jnp.arange(rows * top), side="right").astype(jnp.int32)
    table = members.reshape(top, rows).T
    table = table[jax.random.permutation(jax.random.fold_in(own, 1), rows)]
    offset_by = jax.random.randint(jax.random.fold_in(own, 2), (rows, 1), 0, top)
    return jnp.take_along_axis(table, (jnp.arange(top)[None, :] + offset_by) % top, axis=1)


def shares(amount, total, reach, skew, full):
    weights = [(1 << 20) // math.isqrt(grade ** skew) + 1 for grade in range(1, amount + 1)]
    largest = reach if full else min(reach, max(-(-total // amount), total * weights[0] // sum(weights)))
    least = 1 if total - largest >= amount - 1 else 0
    given, spare = [largest] + [least] * (amount - 1), total - largest - least * (amount - 1)
    while spare > 0:
        free = [i for i in range(1, amount) if given[i] < largest] or [i for i in range(1, amount) if given[i] < reach]
        pool, budget = sum([weights[i] for i in free]), spare
        for i in free:
            extra = min(reach - given[i], max(1, budget * weights[i] // pool), spare)
            given[i] = given[i] + extra
            spare = spare - extra
    return np.array(given)


def scatter_about(key, dims, deviation, limit, pieces=(), kind=jnp.bfloat16):
    gain = block_levels(key, dims, pieces, -0.22, 0.18) if pieces else 1.0
    drawn = jax.random.normal(key, dims, jnp.float32) * deviation * gain
    return jnp.minimum(jnp.maximum(drawn, -limit), limit).astype(kind)


def setup_inputs(seed: int = 0, part: int = 0) -> dict:
    seeds = jax.random.split(jax.random.key(seed), 8)
    own_keys = jax.random.split(jax.random.fold_in(seeds[7], part), 8)
    tokens = scatter_about(own_keys[0], (TOKENS, D), 1.0, 6.0, ((0, 16),))
    parents = draw_parents(jax.random.fold_in(jax.random.fold_in(seeds[7], part), 71), part)
    expert_ids_keys = jax.random.split(jax.random.fold_in(own_keys[2], 1), TOKENS // TOK_DEV)
    expert_ids_turns = jax.random.permutation(jax.random.fold_in(own_keys[2], 3), TOKENS // TOK_DEV)
    expert_ids = jax.vmap(lambda own, number: assign_block(jax.random.fold_in(own_keys[2], 2), own, number, TOK_DEV, EXPERTS, TOP, CAP, 2))(expert_ids_keys, expert_ids_turns).reshape((TOKENS, TOP))
    route_weights = jnp.clip(jnp.exp(math.log(2.0) - 2.3025851 * jax.random.uniform(own_keys[3], (TOKENS, TOP), jnp.float32) ** block_levels(own_keys[3], (TOKENS, TOP), ((0, 16),), -0.2, 0.2)), 0.2, 2.0)
    w_gate = scatter_about(seeds[4], (EXPERTS * SLICES, D, FF_DEV), D ** -0.5, 0.0625, ((0, 16),))
    w_up = scatter_about(seeds[5], (EXPERTS * SLICES, D, FF_DEV), D ** -0.5, 0.0625, ((0, 16),))
    w_down = scatter_about(seeds[6], (EXPERTS * SLICES, FF_DEV, D), FF ** -0.5, 0.125, ((0, 16),))
    return dict(tokens=tokens, parents=parents, expert_ids=expert_ids, route_weights=route_weights, w_gate=w_gate, w_up=w_up, w_down=w_down)


def reference(tokens, parents, expert_ids, route_weights, w_gate, w_up, w_down):
    count = tokens.shape[0]
    base = jnp.arange(count, dtype=jnp.int32) // TOK_DEV * TOK_DEV
    valid = parents >= 0
    index = jnp.where(valid, base + parents, 0).astype(jnp.int32)
    lifted = tokens.astype(jnp.float32) + jnp.where(valid[:, None], tokens[index].astype(jnp.float32), 0.0)
    normed = (lifted * lax.rsqrt(lax.optimization_barrier(jnp.mean(lifted * lifted, axis=1, keepdims=True)) + 1e-06)).astype(jnp.bfloat16)
    gate_all = w_gate.reshape(EXPERTS, SLICES, D, FF_DEV)
    up_all = w_up.reshape(EXPERTS, SLICES, D, FF_DEV)
    down_all = w_down.reshape(EXPERTS, SLICES, FF_DEV, D)
    experts_iota = jnp.arange(EXPERTS, dtype=jnp.int32)
    coef = lax.optimization_barrier(jnp.sum(jnp.where(expert_ids[:, :, None] == experts_iota[None, None, :], route_weights[:, :, None], 0.0), axis=1))
    chosen = jnp.any(expert_ids[:, :, None] == experts_iota[None, None, :], axis=1).astype(jnp.int32)
    room = min(count, N_EP * CAP)

    def one_expert(total, packed):
        gate_w, up_w, down_w, weight_col, chosen_col = packed
        order = jnp.argsort(1 - chosen_col, stable=True)[:room].astype(jnp.int32)
        rows = normed[order]
        weight_rows = weight_col[order]
        gate_m = jnp.transpose(gate_w, (1, 0, 2)).reshape(D, SLICES * FF_DEV)
        up_m = jnp.transpose(up_w, (1, 0, 2)).reshape(D, SLICES * FF_DEV)
        gate = jnp.dot(rows, gate_m, preferred_element_type=jnp.float32)
        upper = jnp.dot(rows, up_m, preferred_element_type=jnp.float32)
        hidden = (jax.nn.silu(gate) * upper).astype(jnp.bfloat16)
        result = jnp.zeros((room, D), jnp.float32)
        for s in range(SLICES):
            piece = jnp.dot(hidden[:, s * FF_DEV:(s + 1) * FF_DEV], down_w[s], preferred_element_type=jnp.float32)
            result = result + piece.astype(jnp.bfloat16).astype(jnp.float32)
        return (total.at[order].add(weight_rows[:, None] * result), None)
    total, unused = lax.scan(one_expert, jnp.zeros((count, D), jnp.float32), (gate_all, up_all, down_all, coef.T, chosen.T))
    return total.astype(jnp.bfloat16)
```

```python
import jax
import jax.numpy as jnp
from jax import lax
from jax.sharding import Mesh
from jax.sharding import PartitionSpec as P

SLICES = 8


def slice_ffn(rows, gate_w, up_w, down_w):
    gate = jnp.dot(rows, gate_w, preferred_element_type=jnp.float32)
    upper = jnp.dot(rows, up_w, preferred_element_type=jnp.float32)
    hidden = (jax.nn.silu(gate) * upper).astype(jnp.bfloat16)
    return jnp.dot(hidden, down_w, preferred_element_type=jnp.float32).astype(jnp.bfloat16)


def shards(tokens, parents, expert_ids, route_weights, w_gate, w_up, w_down):
    count, width = tokens.shape
    picks_row = expert_ids.shape[1]
    experts = lax.axis_size("eg")
    slices = lax.axis_size("sl")
    slots = 5 * count * picks_row // (4 * experts)
    nodes = jnp.arange(count, dtype=jnp.int32)
    parent_hot = (parents[:, None] == nodes[None, :]).astype(jnp.bfloat16)
    lifted = tokens.astype(jnp.float32) + jnp.dot(
        parent_hot, tokens, preferred_element_type=jnp.float32
    )
    normed = (lifted * lax.rsqrt(jnp.mean(lifted * lifted, axis=1, keepdims=True) + 1e-06)).astype(
        jnp.bfloat16
    )
    picks = expert_ids[:, :, None] == jnp.arange(experts, dtype=jnp.int32)[None, None, :]
    chosen = jnp.any(picks, axis=1).astype(jnp.int32)
    before = jnp.cumsum(chosen, axis=0) - chosen
    slot_iota = jnp.arange(slots, dtype=jnp.int32)
    place = (chosen[:, :, None] * (before[:, :, None] == slot_iota[None, None, :])) > 0
    weight_te = jnp.sum(jnp.where(picks, route_weights[:, :, None], 0.0), axis=1)
    packed = jnp.einsum(
        "tec,td->ecd", place.astype(jnp.bfloat16), normed, preferred_element_type=jnp.float32
    ).astype(jnp.bfloat16)
    packed_w = jnp.sum(jnp.where(place, weight_te[:, :, None], 0.0), axis=0)
    mine = lax.all_to_all(packed, "eg", split_axis=0, concat_axis=0, tiled=True)
    mine_w = lax.all_to_all(packed_w, "eg", split_axis=0, concat_axis=0, tiled=True)
    held = mine.reshape(experts * slots, width)
    gathered = lax.all_gather(held, "sl", axis=0, tiled=True)
    parts = slice_ffn(gathered, w_gate[0], w_up[0], w_down[0])
    back = lax.all_to_all(
        parts.reshape(slices, experts * slots, width), "sl", split_axis=0, concat_axis=0, tiled=True
    )
    summed = jnp.sum(back.astype(jnp.float32), axis=0)
    weighted = (summed * mine_w.reshape(experts * slots, 1)).astype(jnp.bfloat16)
    home = lax.all_to_all(
        weighted.reshape(experts, slots, width), "eg", split_axis=0, concat_axis=0, tiled=True
    )
    result = jnp.einsum(
        "tec,ecd->td", place.astype(jnp.bfloat16), home, preferred_element_type=jnp.float32
    )
    return result.astype(jnp.bfloat16)


def solution(mesh):
    groups, ranks = mesh.devices.shape
    experts = ranks // SLICES
    split = Mesh(mesh.devices.reshape(groups, experts, SLICES), ("grp", "eg", "sl"))
    rows = ("grp", "eg", "sl")
    placed = (
        P(rows, None),
        P(rows),
        P(rows, None),
        P(rows, None),
        P(("eg", "sl"), None, None),
        P(("eg", "sl"), None, None),
        P(("eg", "sl"), None, None),
    )
    return jax.shard_map(
        shards, mesh=split, in_specs=placed, out_specs=P(rows, None), check_vma=False
    )
```

```python
import jax
import jax.numpy as jnp
from jax import lax
from jax.sharding import Mesh
from jax.sharding import PartitionSpec as P

SLICES = 8


def slice_ffn(rows, gate_w, up_w, down_w):
    gate = jnp.dot(rows, gate_w, preferred_element_type=jnp.float32)
    upper = jnp.dot(rows, up_w, preferred_element_type=jnp.float32)
    hidden = (jax.nn.silu(gate) * upper).astype(jnp.bfloat16)
    return jnp.dot(hidden, down_w, preferred_element_type=jnp.float32).astype(jnp.bfloat16)


def shards(tokens, parents, expert_ids, route_weights, w_gate, w_up, w_down):
    count, width = tokens.shape
    picks_row = expert_ids.shape[1]
    experts = lax.axis_size("eg")
    chips = lax.axis_size("sc")
    cores = lax.axis_size("core")
    slots = 5 * count * picks_row // (4 * experts)
    nodes = jnp.arange(count, dtype=jnp.int32)
    parent_hot = (parents[:, None] == nodes[None, :]).astype(jnp.bfloat16)
    lifted = tokens.astype(jnp.float32) + jnp.dot(
        parent_hot, tokens, preferred_element_type=jnp.float32
    )
    normed = (lifted * lax.rsqrt(jnp.mean(lifted * lifted, axis=1, keepdims=True) + 1e-06)).astype(
        jnp.bfloat16
    )
    picks = expert_ids[:, :, None] == jnp.arange(experts, dtype=jnp.int32)[None, None, :]
    chosen = jnp.any(picks, axis=1).astype(jnp.int32)
    before = jnp.cumsum(chosen, axis=0) - chosen
    slot_iota = jnp.arange(slots, dtype=jnp.int32)
    place = (chosen[:, :, None] * (before[:, :, None] == slot_iota[None, None, :])) > 0
    weight_te = jnp.sum(jnp.where(picks, route_weights[:, :, None], 0.0), axis=1)
    packed = jnp.einsum(
        "tec,td->ecd", place.astype(jnp.bfloat16), normed, preferred_element_type=jnp.float32
    ).astype(jnp.bfloat16)
    packed_w = jnp.sum(jnp.where(place, weight_te[:, :, None], 0.0), axis=0)
    mine = lax.all_to_all(packed, "eg", split_axis=0, concat_axis=0, tiled=True)
    mine_w = lax.all_to_all(packed_w, "eg", split_axis=0, concat_axis=0, tiled=True)
    held = mine.reshape(experts * slots, width)
    gathered = lax.all_gather(held, ("core", "sc"), axis=0, tiled=True)
    parts = slice_ffn(gathered, w_gate[0], w_up[0], w_down[0])
    paired = lax.psum_scatter(
        parts.reshape(cores, chips * experts * slots, width), "core", scatter_dimension=0, tiled=True
    )
    back = lax.all_to_all(
        paired.reshape(chips, experts * slots, width), "sc", split_axis=0, concat_axis=0, tiled=True
    )
    summed = jnp.sum(back.astype(jnp.float32), axis=0)
    weighted = (summed * mine_w.reshape(experts * slots, 1)).astype(jnp.bfloat16)
    home = lax.all_to_all(
        weighted.reshape(experts, slots, width), "eg", split_axis=0, concat_axis=0, tiled=True
    )
    result = jnp.einsum(
        "tec,ecd->td", place.astype(jnp.bfloat16), home, preferred_element_type=jnp.float32
    )
    return result.astype(jnp.bfloat16)


def solution(mesh):
    groups, ranks = mesh.devices.shape
    experts = ranks // SLICES
    cores = 2
    split = Mesh(
        mesh.devices.reshape(groups, experts, SLICES // cores, cores), ("grp", "eg", "sc", "core")
    )
    rows = ("grp", "eg", "sc", "core")
    placed = (
        P(rows, None),
        P(rows),
        P(rows, None),
        P(rows, None),
        P(("eg", "sc", "core"), None, None),
        P(("eg", "sc", "core"), None, None),
        P(("eg", "sc", "core"), None, None),
    )
    return jax.shard_map(
        shards, mesh=split, in_specs=placed, out_specs=P(rows, None), check_vma=False
    )
```

```python
import jax
import jax.numpy as jnp
from jax import lax
from jax.sharding import Mesh
from jax.sharding import PartitionSpec as P

SLICES = 8


def slice_ffn(rows, gate_w, up_w, down_w):
    gate = jnp.dot(rows, gate_w, preferred_element_type=jnp.float32)
    upper = jnp.dot(rows, up_w, preferred_element_type=jnp.float32)
    hidden = (jax.nn.silu(gate) * upper).astype(jnp.bfloat16)
    return jnp.dot(hidden, down_w, preferred_element_type=jnp.float32).astype(jnp.bfloat16)


def expert_rows(held, weights, gate_w, up_w, down_w):
    chips = lax.axis_size("sc")
    cores = lax.axis_size("core")
    count, width = held.shape
    gathered = lax.all_gather(held, ("core", "sc"), axis=0, tiled=True)
    parts = slice_ffn(gathered, gate_w, up_w, down_w)
    paired = lax.psum_scatter(
        parts.reshape(cores, chips * count, width), "core", scatter_dimension=0, tiled=True
    )
    back = lax.all_to_all(
        paired.reshape(chips, count, width), "sc", split_axis=0, concat_axis=0, tiled=True
    )
    summed = jnp.sum(back.astype(jnp.float32), axis=0)
    return (summed * weights[:, None]).astype(jnp.bfloat16)


def shards(tokens, parents, expert_ids, route_weights, w_gate, w_up, w_down):
    count, width = tokens.shape
    picks_row = expert_ids.shape[1]
    experts = lax.axis_size("eg")
    group = lax.axis_index("eg")
    slots = 5 * count * picks_row // (4 * experts)
    nodes = jnp.arange(count, dtype=jnp.int32)
    parent_hot = (parents[:, None] == nodes[None, :]).astype(jnp.bfloat16)
    lifted = tokens.astype(jnp.float32) + jnp.dot(
        parent_hot, tokens, preferred_element_type=jnp.float32
    )
    normed = (lifted * lax.rsqrt(jnp.mean(lifted * lifted, axis=1, keepdims=True) + 1e-06)).astype(
        jnp.bfloat16
    )
    relative = (expert_ids - group) % experts
    picks = relative[:, :, None] == jnp.arange(experts, dtype=jnp.int32)[None, None, :]
    chosen = jnp.any(picks, axis=1).astype(jnp.int32)
    before = jnp.cumsum(chosen, axis=0) - chosen
    slot_iota = jnp.arange(slots, dtype=jnp.int32)
    place = (chosen[:, :, None] * (before[:, :, None] == slot_iota[None, None, :])) > 0
    weight_te = jnp.sum(jnp.where(picks, route_weights[:, :, None], 0.0), axis=1)
    packed = jnp.einsum(
        "tkc,td->kcd", place.astype(jnp.bfloat16), normed, preferred_element_type=jnp.float32
    ).astype(jnp.bfloat16)
    packed_w = jnp.sum(jnp.where(place, weight_te[:, :, None], 0.0), axis=0)
    weights = (w_gate[0], w_up[0], w_down[0])

    def shift(k):
        return [(g, (g + k) % experts) for g in range(experts)]

    away = [lax.ppermute(packed[k], "eg", shift(k)) for k in range(1, experts)]
    away_w = [lax.ppermute(packed_w[k], "eg", shift(k)) for k in range(1, experts)]
    own = expert_rows(packed[0], packed_w[0], *weights)
    done = expert_rows(
        jnp.concatenate(away, axis=0), jnp.concatenate(away_w, axis=0), *weights
    )
    home = [own] + [
        lax.ppermute(done[(k - 1) * slots:k * slots], "eg", shift(experts - k))
        for k in range(1, experts)
    ]
    result = jnp.einsum(
        "tkc,kcd->td",
        place.astype(jnp.bfloat16),
        jnp.stack(home),
        preferred_element_type=jnp.float32,
    )
    return result.astype(jnp.bfloat16)


def solution(mesh):
    groups, ranks = mesh.devices.shape
    experts = ranks // SLICES
    cores = 2
    split = Mesh(
        mesh.devices.reshape(groups, experts, SLICES // cores, cores), ("grp", "eg", "sc", "core")
    )
    rows = ("grp", "eg", "sc", "core")
    placed = (
        P(rows, None),
        P(rows),
        P(rows, None),
        P(rows, None),
        P(("eg", "sc", "core"), None, None),
        P(("eg", "sc", "core"), None, None),
        P(("eg", "sc", "core"), None, None),
    )
    return jax.shard_map(
        shards, mesh=split, in_specs=placed, out_specs=P(rows, None), check_vma=False
    )
```

```python
import jax
import jax.numpy as jnp
from jax import lax
from jax.sharding import Mesh
from jax.sharding import PartitionSpec as P

SLICES = 8


def slice_ffn(rows, gate_w, up_w, down_w):
    gate = jnp.dot(rows, gate_w, preferred_element_type=jnp.float32)
    upper = jnp.dot(rows, up_w, preferred_element_type=jnp.float32)
    hidden = (jax.nn.silu(gate) * upper).astype(jnp.bfloat16)
    return jnp.dot(hidden, down_w, preferred_element_type=jnp.float32).astype(jnp.bfloat16)


def expert_rows(held, weights, gate_w, up_w, down_w):
    chips = lax.axis_size("sc")
    cores = lax.axis_size("core")
    count, width = held.shape
    gathered = lax.all_gather(held, ("core", "sc"), axis=0, tiled=True)
    parts = slice_ffn(gathered, gate_w, up_w, down_w)
    halves = parts.reshape(cores, chips * count, width)
    core = lax.axis_index("core")
    swap = [(c, (c + 1) % cores) for c in range(cores)]
    sibling = lax.ppermute(halves[(core + 1) % cores], "core", swap)
    paired = (halves[core].astype(jnp.float32) + sibling.astype(jnp.float32)).astype(jnp.bfloat16)
    back = lax.all_to_all(
        paired.reshape(chips, count, width), "sc", split_axis=0, concat_axis=0, tiled=True
    )
    summed = jnp.sum(back.astype(jnp.float32), axis=0)
    return (summed * weights[:, None]).astype(jnp.bfloat16)


def shards(tokens, parents, expert_ids, route_weights, w_gate, w_up, w_down):
    count, width = tokens.shape
    picks_row = expert_ids.shape[1]
    experts = lax.axis_size("eg")
    group = lax.axis_index("eg")
    slots = 5 * count * picks_row // (4 * experts)
    nodes = jnp.arange(count, dtype=jnp.int32)
    parent_hot = (parents[:, None] == nodes[None, :]).astype(jnp.bfloat16)
    lifted = tokens.astype(jnp.float32) + jnp.dot(
        parent_hot, tokens, preferred_element_type=jnp.float32
    )
    normed = (lifted * lax.rsqrt(jnp.mean(lifted * lifted, axis=1, keepdims=True) + 1e-06)).astype(
        jnp.bfloat16
    )
    relative = (expert_ids - group) % experts
    picks = relative[:, :, None] == jnp.arange(experts, dtype=jnp.int32)[None, None, :]
    chosen = jnp.any(picks, axis=1).astype(jnp.int32)
    before = jnp.cumsum(chosen, axis=0) - chosen
    slot_iota = jnp.arange(slots, dtype=jnp.int32)
    place = (chosen[:, :, None] * (before[:, :, None] == slot_iota[None, None, :])) > 0
    weight_te = jnp.sum(jnp.where(picks, route_weights[:, :, None], 0.0), axis=1)
    packed = jnp.einsum(
        "tkc,td->kcd", place.astype(jnp.bfloat16), normed, preferred_element_type=jnp.float32
    ).astype(jnp.bfloat16)
    packed_w = jnp.sum(jnp.where(place, weight_te[:, :, None], 0.0), axis=0)
    weights = (w_gate[0], w_up[0], w_down[0])

    def shift(k):
        return [(g, (g + k) % experts) for g in range(experts)]

    away = [lax.ppermute(packed[k], "eg", shift(k)) for k in range(1, experts)]
    away_w = [lax.ppermute(packed_w[k], "eg", shift(k)) for k in range(1, experts)]
    own = expert_rows(packed[0], packed_w[0], *weights)
    done = expert_rows(
        jnp.concatenate(away, axis=0), jnp.concatenate(away_w, axis=0), *weights
    )
    home = [own] + [
        lax.ppermute(done[(k - 1) * slots:k * slots], "eg", shift(experts - k))
        for k in range(1, experts)
    ]
    result = jnp.einsum(
        "tkc,kcd->td",
        place.astype(jnp.bfloat16),
        jnp.stack(home),
        preferred_element_type=jnp.float32,
    )
    return result.astype(jnp.bfloat16)


def solution(mesh):
    groups, ranks = mesh.devices.shape
    experts = ranks // SLICES
    cores = 2
    split = Mesh(
        mesh.devices.reshape(groups, experts, SLICES // cores, cores), ("grp", "eg", "sc", "core")
    )
    rows = ("grp", "eg", "sc", "core")
    placed = (
        P(rows, None),
        P(rows),
        P(rows, None),
        P(rows, None),
        P(("eg", "sc", "core"), None, None),
        P(("eg", "sc", "core"), None, None),
        P(("eg", "sc", "core"), None, None),
    )
    return jax.shard_map(
        shards, mesh=split, in_specs=placed, out_specs=P(rows, None), check_vma=False
    )
```

```python
import jax
import jax.numpy as jnp
from jax import lax
from jax.sharding import Mesh
from jax.sharding import PartitionSpec as P

SLICES = 8


def slice_ffn(rows, gate_w, up_w, down_w):
    gate = jnp.dot(rows, gate_w, preferred_element_type=jnp.float32)
    upper = jnp.dot(rows, up_w, preferred_element_type=jnp.float32)
    hidden = (jax.nn.silu(gate) * upper).astype(jnp.bfloat16)
    return jnp.dot(hidden, down_w, preferred_element_type=jnp.float32).astype(jnp.bfloat16)


def gather(held):
    return lax.all_gather(held, ("core", "sc"), axis=0, tiled=True)


def expert_parts(gathered, gate_w, up_w, down_w):
    chips = lax.axis_size("sc")
    cores = lax.axis_size("core")
    count = gathered.shape[0] // (chips * cores)
    width = gathered.shape[1]
    parts = slice_ffn(gathered, gate_w, up_w, down_w)
    halves = parts.reshape(cores, chips * count, width)
    core = lax.axis_index("core")
    swap = [(c, (c + 1) % cores) for c in range(cores)]
    sibling = lax.ppermute(halves[(core + 1) % cores], "core", swap)
    paired = (halves[core].astype(jnp.float32) + sibling.astype(jnp.float32)).astype(jnp.bfloat16)
    return paired.reshape(chips, count, width)


def chip_sums(paired):
    return lax.all_to_all(paired, "sc", split_axis=0, concat_axis=0, tiled=True)


def finish(back, weights):
    summed = jnp.sum(back.astype(jnp.float32), axis=0)
    return (summed * weights[:, None]).astype(jnp.bfloat16)


def shards(tokens, parents, expert_ids, route_weights, w_gate, w_up, w_down):
    count, width = tokens.shape
    picks_row = expert_ids.shape[1]
    experts = lax.axis_size("eg")
    group = lax.axis_index("eg")
    slots = 5 * count * picks_row // (4 * experts)
    nodes = jnp.arange(count, dtype=jnp.int32)
    parent_hot = (parents[:, None] == nodes[None, :]).astype(jnp.bfloat16)
    lifted = tokens.astype(jnp.float32) + jnp.dot(
        parent_hot, tokens, preferred_element_type=jnp.float32
    )
    normed = (lifted * lax.rsqrt(jnp.mean(lifted * lifted, axis=1, keepdims=True) + 1e-06)).astype(
        jnp.bfloat16
    )
    relative = (expert_ids - group) % experts
    picks = relative[:, :, None] == jnp.arange(experts, dtype=jnp.int32)[None, None, :]
    chosen = jnp.any(picks, axis=1).astype(jnp.int32)
    before = jnp.cumsum(chosen, axis=0) - chosen
    slot_iota = jnp.arange(slots, dtype=jnp.int32)
    place = (chosen[:, :, None] * (before[:, :, None] == slot_iota[None, None, :])) > 0
    weight_te = jnp.sum(jnp.where(picks, route_weights[:, :, None], 0.0), axis=1)
    packed = jnp.einsum(
        "tkc,td->kcd", place.astype(jnp.bfloat16), normed, preferred_element_type=jnp.float32
    ).astype(jnp.bfloat16)
    packed_w = jnp.sum(jnp.where(place, weight_te[:, :, None], 0.0), axis=0)
    weights = (w_gate[0], w_up[0], w_down[0])

    def shift(k):
        return [(g, (g + k) % experts) for g in range(experts)]

    away = [lax.ppermute(packed[k], "eg", shift(k)) for k in range(1, experts)]
    away_w = [lax.ppermute(packed_w[k], "eg", shift(k)) for k in range(1, experts)]
    own_rows = gather(packed[0])
    own_rows, away = lax.optimization_barrier((own_rows, away))
    own_parts = expert_parts(own_rows, *weights)
    away_parts = expert_parts(gather(jnp.concatenate(away, axis=0)), *weights)
    away_back = chip_sums(away_parts)
    own_parts, away_back = lax.optimization_barrier((own_parts, away_back))
    done = finish(away_back, jnp.concatenate(away_w, axis=0))
    own = finish(chip_sums(own_parts), packed_w[0])
    home = [own] + [
        lax.ppermute(done[(k - 1) * slots:k * slots], "eg", shift(experts - k))
        for k in range(1, experts)
    ]
    result = jnp.einsum(
        "tkc,kcd->td",
        place.astype(jnp.bfloat16),
        jnp.stack(home),
        preferred_element_type=jnp.float32,
    )
    return result.astype(jnp.bfloat16)


def solution(mesh):
    groups, ranks = mesh.devices.shape
    experts = ranks // SLICES
    cores = 2
    split = Mesh(
        mesh.devices.reshape(groups, experts, SLICES // cores, cores), ("grp", "eg", "sc", "core")
    )
    rows = ("grp", "eg", "sc", "core")
    placed = (
        P(rows, None),
        P(rows),
        P(rows, None),
        P(rows, None),
        P(("eg", "sc", "core"), None, None),
        P(("eg", "sc", "core"), None, None),
        P(("eg", "sc", "core"), None, None),
    )
    return jax.shard_map(
        shards, mesh=split, in_specs=placed, out_specs=P(rows, None), check_vma=False
    )
```

```python
import jax
import jax.numpy as jnp
from jax import lax
from jax.sharding import Mesh
from jax.sharding import PartitionSpec as P

SLICES = 8


def slice_ffn(rows, gate_w, up_w, down_w):
    gate = jnp.dot(rows, gate_w, preferred_element_type=jnp.float32)
    upper = jnp.dot(rows, up_w, preferred_element_type=jnp.float32)
    hidden = (jax.nn.silu(gate) * upper).astype(jnp.bfloat16)
    return jnp.dot(hidden, down_w, preferred_element_type=jnp.float32).astype(jnp.bfloat16)


def gather(held):
    return lax.all_gather(held, ("core", "sc"), axis=0, tiled=True)


def expert_parts(gathered, gate_w, up_w, down_w):
    chips = lax.axis_size("sc")
    cores = lax.axis_size("core")
    count = gathered.shape[0] // (chips * cores)
    width = gathered.shape[1]
    parts = slice_ffn(gathered, gate_w, up_w, down_w)
    halves = parts.reshape(cores, chips * count, width)
    core = lax.axis_index("core")
    swap = [(c, (c + 1) % cores) for c in range(cores)]
    sibling = lax.ppermute(halves[(core + 1) % cores], "core", swap)
    paired = (halves[core].astype(jnp.float32) + sibling.astype(jnp.float32)).astype(jnp.bfloat16)
    return paired.reshape(chips, count, width)


def chip_sums(paired):
    return lax.all_to_all(paired, "sc", split_axis=0, concat_axis=0, tiled=True)


def finish(back, weights):
    summed = jnp.sum(back.astype(jnp.float32), axis=0)
    return (summed * weights[:, None]).astype(jnp.bfloat16)


def shards(tokens, parents, expert_ids, route_weights, w_gate, w_up, w_down):
    count, width = tokens.shape
    picks_row = expert_ids.shape[1]
    experts = lax.axis_size("eg")
    group = lax.axis_index("eg")
    slots = 5 * count * picks_row // (4 * experts)
    nodes = jnp.arange(count, dtype=jnp.int32)
    parent_hot = (parents[:, None] == nodes[None, :]).astype(jnp.bfloat16)
    lifted = tokens.astype(jnp.float32) + jnp.dot(
        parent_hot, tokens, preferred_element_type=jnp.float32
    )
    normed = (lifted * lax.rsqrt(jnp.mean(lifted * lifted, axis=1, keepdims=True) + 1e-06)).astype(
        jnp.bfloat16
    )
    relative = (expert_ids - group) % experts
    picks = relative[:, :, None] == jnp.arange(experts, dtype=jnp.int32)[None, None, :]
    chosen = jnp.any(picks, axis=1).astype(jnp.int32)
    before = jnp.cumsum(chosen, axis=0) - chosen
    slot_iota = jnp.arange(slots, dtype=jnp.int32)
    place = (chosen[:, :, None] * (before[:, :, None] == slot_iota[None, None, :])) > 0
    weight_te = jnp.sum(jnp.where(picks, route_weights[:, :, None], 0.0), axis=1)
    packed = jnp.einsum(
        "tkc,td->kcd", place.astype(jnp.bfloat16), normed, preferred_element_type=jnp.float32
    ).astype(jnp.bfloat16)
    packed_w = jnp.sum(jnp.where(place, weight_te[:, :, None], 0.0), axis=0)
    weights = (w_gate[0], w_up[0], w_down[0])

    def shift(k):
        return [(g, (g + k) % experts) for g in range(experts)]

    away = [lax.ppermute(packed[k], "eg", shift(k)) for k in range(1, experts)]
    away_w = [lax.ppermute(packed_w[k], "eg", shift(k)) for k in range(1, experts)]
    own_rows = gather(packed[0])
    own_rows, away, away_w = lax.optimization_barrier((own_rows, away, away_w))
    own_parts = expert_parts(own_rows, *weights)
    away_parts = expert_parts(gather(jnp.concatenate(away, axis=0)), *weights)
    away_back = chip_sums(away_parts)
    own_parts, away_back = lax.optimization_barrier((own_parts, away_back))
    done = finish(away_back, jnp.concatenate(away_w, axis=0))
    own = finish(chip_sums(own_parts), packed_w[0])
    home = [own] + [
        lax.ppermute(done[(k - 1) * slots:k * slots], "eg", shift(experts - k))
        for k in range(1, experts)
    ]
    result = jnp.einsum(
        "tkc,kcd->td",
        place.astype(jnp.bfloat16),
        jnp.stack(home),
        preferred_element_type=jnp.float32,
    )
    return result.astype(jnp.bfloat16)


def solution(mesh):
    groups, ranks = mesh.devices.shape
    experts = ranks // SLICES
    cores = 2
    split = Mesh(
        mesh.devices.reshape(groups, experts, SLICES // cores, cores), ("grp", "eg", "sc", "core")
    )
    rows = ("grp", "eg", "sc", "core")
    placed = (
        P(rows, None),
        P(rows),
        P(rows, None),
        P(rows, None),
        P(("eg", "sc", "core"), None, None),
        P(("eg", "sc", "core"), None, None),
        P(("eg", "sc", "core"), None, None),
    )
    return jax.shard_map(
        shards, mesh=split, in_specs=placed, out_specs=P(rows, None), check_vma=False
    )
```

```python
import jax
import jax.numpy as jnp
from jax import lax
from jax.sharding import Mesh
from jax.sharding import PartitionSpec as P

SLICES = 8


def slice_ffn(rows, gate_w, up_w, down_w):
    gate = jnp.dot(rows, gate_w, preferred_element_type=jnp.float32)
    upper = jnp.dot(rows, up_w, preferred_element_type=jnp.float32)
    hidden = (jax.nn.silu(gate) * upper).astype(jnp.bfloat16)
    return jnp.dot(hidden, down_w, preferred_element_type=jnp.float32).astype(jnp.bfloat16)


def gather(held):
    return lax.all_gather(held, ("core", "sc"), axis=0, tiled=True)


def expert_parts(gathered, gate_w, up_w, down_w):
    chips = lax.axis_size("sc")
    cores = lax.axis_size("core")
    count = gathered.shape[0] // (chips * cores)
    width = gathered.shape[1]
    parts = slice_ffn(gathered, gate_w, up_w, down_w)
    halves = parts.reshape(cores, chips * count, width)
    core = lax.axis_index("core")
    swap = [(c, (c + 1) % cores) for c in range(cores)]
    sibling = lax.ppermute(halves[(core + 1) % cores], "core", swap)
    paired = (halves[core].astype(jnp.float32) + sibling.astype(jnp.float32)).astype(jnp.bfloat16)
    return paired.reshape(chips, count, width)


def chip_sums(paired):
    return lax.all_to_all(paired, "sc", split_axis=0, concat_axis=0, tiled=True)


def finish(back, weights):
    summed = jnp.sum(back.astype(jnp.float32), axis=0)
    return (summed * weights[:, None]).astype(jnp.bfloat16)


def shards(tokens, parents, expert_ids, route_weights, w_gate, w_up, w_down):
    count, width = tokens.shape
    picks_row = expert_ids.shape[1]
    experts = lax.axis_size("eg")
    group = lax.axis_index("eg")
    slots = 5 * count * picks_row // (4 * experts)
    nodes = jnp.arange(count, dtype=jnp.int32)
    parent_hot = (parents[:, None] == nodes[None, :]).astype(jnp.bfloat16)
    lifted = tokens.astype(jnp.float32) + jnp.dot(
        parent_hot, tokens, preferred_element_type=jnp.float32
    )
    normed = (lifted * lax.rsqrt(jnp.mean(lifted * lifted, axis=1, keepdims=True) + 1e-06)).astype(
        jnp.bfloat16
    )
    relative = (expert_ids - group) % experts
    picks = relative[:, :, None] == jnp.arange(experts, dtype=jnp.int32)[None, None, :]
    chosen = jnp.any(picks, axis=1).astype(jnp.int32)
    before = jnp.cumsum(chosen, axis=0) - chosen
    slot_iota = jnp.arange(slots, dtype=jnp.int32)
    place = (chosen[:, :, None] * (before[:, :, None] == slot_iota[None, None, :])) > 0
    weight_te = jnp.sum(jnp.where(picks, route_weights[:, :, None], 0.0), axis=1)
    packed = jnp.einsum(
        "tkc,td->kcd", place.astype(jnp.bfloat16), normed, preferred_element_type=jnp.float32
    ).astype(jnp.bfloat16)
    packed_w = jnp.sum(jnp.where(place, weight_te[:, :, None], 0.0), axis=0)
    weights = (w_gate[0], w_up[0], w_down[0])

    def shift(k):
        return [(g, (g + k) % experts) for g in range(experts)]

    away = [lax.ppermute(packed[k], "eg", shift(k)) for k in range(1, experts)]
    away_w = [lax.ppermute(packed_w[k], "eg", shift(k)) for k in range(1, experts)]
    own_rows = gather(packed[0])
    own_rows, away, away_w = lax.optimization_barrier((own_rows, away, away_w))
    own_parts = expert_parts(own_rows, *weights)
    away_rows = gather(jnp.concatenate(away, axis=0))
    own_parts, away_rows = lax.optimization_barrier((own_parts, away_rows))
    away_parts = expert_parts(away_rows, *weights)
    away_back = chip_sums(away_parts)
    own_parts, away_back = lax.optimization_barrier((own_parts, away_back))
    done = finish(away_back, jnp.concatenate(away_w, axis=0))
    own = finish(chip_sums(own_parts), packed_w[0])
    home = [own] + [
        lax.ppermute(done[(k - 1) * slots:k * slots], "eg", shift(experts - k))
        for k in range(1, experts)
    ]
    result = jnp.einsum(
        "tkc,kcd->td",
        place.astype(jnp.bfloat16),
        jnp.stack(home),
        preferred_element_type=jnp.float32,
    )
    return result.astype(jnp.bfloat16)


def solution(mesh):
    groups, ranks = mesh.devices.shape
    experts = ranks // SLICES
    cores = 2
    split = Mesh(
        mesh.devices.reshape(groups, experts, SLICES // cores, cores), ("grp", "eg", "sc", "core")
    )
    rows = ("grp", "eg", "sc", "core")
    placed = (
        P(rows, None),
        P(rows),
        P(rows, None),
        P(rows, None),
        P(("eg", "sc", "core"), None, None),
        P(("eg", "sc", "core"), None, None),
        P(("eg", "sc", "core"), None, None),
    )
    return jax.shard_map(
        shards, mesh=split, in_specs=placed, out_specs=P(rows, None), check_vma=False
    )
```

```python
import jax
import jax.numpy as jnp
from jax import lax
from jax.sharding import Mesh
from jax.sharding import PartitionSpec as P

SLICES = 8


def slice_ffn(rows, gate_w, up_w, down_w):
    gate = jnp.dot(rows, gate_w, preferred_element_type=jnp.float32)
    upper = jnp.dot(rows, up_w, preferred_element_type=jnp.float32)
    hidden = (jax.nn.silu(gate) * upper).astype(jnp.bfloat16)
    return jnp.dot(hidden, down_w, preferred_element_type=jnp.float32).astype(jnp.bfloat16)


def gather(held):
    return lax.all_gather(held, ("core", "sc"), axis=0, tiled=True)


def expert_parts(gathered, gate_w, up_w, down_w):
    chips = lax.axis_size("sc")
    cores = lax.axis_size("core")
    count = gathered.shape[0] // (chips * cores)
    width = gathered.shape[1]
    parts = slice_ffn(gathered, gate_w, up_w, down_w)
    halves = parts.reshape(cores, chips * count, width)
    core = lax.axis_index("core")
    swap = [(c, (c + 1) % cores) for c in range(cores)]
    sibling = lax.ppermute(halves[(core + 1) % cores], "core", swap)
    paired = (halves[core].astype(jnp.float32) + sibling.astype(jnp.float32)).astype(jnp.bfloat16)
    return paired.reshape(chips, count, width)


def chip_sums(paired):
    return lax.all_to_all(paired, "sc", split_axis=0, concat_axis=0, tiled=True)


def finish(back, weights):
    summed = jnp.sum(back.astype(jnp.float32), axis=0)
    return (summed * weights[:, None]).astype(jnp.bfloat16)


def shards(tokens, parents, expert_ids, route_weights, w_gate, w_up, w_down):
    count, width = tokens.shape
    picks_row = expert_ids.shape[1]
    experts = lax.axis_size("eg")
    group = lax.axis_index("eg")
    slots = 5 * count * picks_row // (4 * experts)
    nodes = jnp.arange(count, dtype=jnp.int32)
    parent_hot = (parents[:, None] == nodes[None, :]).astype(jnp.bfloat16)
    lifted = tokens.astype(jnp.float32) + jnp.dot(
        parent_hot, tokens, preferred_element_type=jnp.float32
    )
    normed = (lifted * lax.rsqrt(jnp.mean(lifted * lifted, axis=1, keepdims=True) + 1e-06)).astype(
        jnp.bfloat16
    )
    relative = (expert_ids - group) % experts
    picks = relative[:, :, None] == jnp.arange(experts, dtype=jnp.int32)[None, None, :]
    chosen = jnp.any(picks, axis=1).astype(jnp.int32)
    before = jnp.cumsum(chosen, axis=0) - chosen
    slot_iota = jnp.arange(slots, dtype=jnp.int32)
    place = (chosen[:, :, None] * (before[:, :, None] == slot_iota[None, None, :])) > 0
    weight_te = jnp.sum(jnp.where(picks, route_weights[:, :, None], 0.0), axis=1)
    packed = jnp.einsum(
        "tkc,td->kcd", place.astype(jnp.bfloat16), normed, preferred_element_type=jnp.float32
    ).astype(jnp.bfloat16)
    packed_w = jnp.sum(jnp.where(place, weight_te[:, :, None], 0.0), axis=0)
    weights = (w_gate[0], w_up[0], w_down[0])

    def shift(k):
        return [(g, (g + k) % experts) for g in range(experts)]

    away = [lax.ppermute(packed[k], "eg", shift(k)) for k in range(1, experts)]
    away_w = [lax.ppermute(packed_w[k], "eg", shift(k)) for k in range(1, experts)]
    own_rows = gather(packed[0])
    own_rows, away, away_w = lax.optimization_barrier((own_rows, away, away_w))
    own_parts = expert_parts(own_rows, *weights)
    away_rows = gather(jnp.concatenate(away, axis=0))
    own_parts, away_rows = lax.optimization_barrier((own_parts, away_rows))
    half = slots // 2
    own_early = chip_sums(own_parts[:, :half])
    away_parts = expert_parts(away_rows, *weights)
    own_early, away_parts = lax.optimization_barrier((own_early, away_parts))
    away_back = chip_sums(away_parts)
    own_late, away_back = lax.optimization_barrier((own_parts[:, half:], away_back))
    done = finish(away_back, jnp.concatenate(away_w, axis=0))
    own_back = jnp.concatenate([own_early, chip_sums(own_late)], axis=1)
    own = finish(own_back, packed_w[0])
    home = [own] + [
        lax.ppermute(done[(k - 1) * slots:k * slots], "eg", shift(experts - k))
        for k in range(1, experts)
    ]
    result = jnp.einsum(
        "tkc,kcd->td",
        place.astype(jnp.bfloat16),
        jnp.stack(home),
        preferred_element_type=jnp.float32,
    )
    return result.astype(jnp.bfloat16)


def solution(mesh):
    groups, ranks = mesh.devices.shape
    experts = ranks // SLICES
    cores = 2
    split = Mesh(
        mesh.devices.reshape(groups, experts, SLICES // cores, cores), ("grp", "eg", "sc", "core")
    )
    rows = ("grp", "eg", "sc", "core")
    placed = (
        P(rows, None),
        P(rows),
        P(rows, None),
        P(rows, None),
        P(("eg", "sc", "core"), None, None),
        P(("eg", "sc", "core"), None, None),
        P(("eg", "sc", "core"), None, None),
    )
    return jax.shard_map(
        shards, mesh=split, in_specs=placed, out_specs=P(rows, None), check_vma=False
    )
```

```python
import jax
import jax.numpy as jnp
from jax import lax
from jax.sharding import Mesh
from jax.sharding import PartitionSpec as P

SLICES = 8


def slice_ffn(rows, gate_w, up_w, down_w):
    gate = jnp.dot(rows, gate_w, preferred_element_type=jnp.float32)
    upper = jnp.dot(rows, up_w, preferred_element_type=jnp.float32)
    hidden = (jax.nn.silu(gate) * upper).astype(jnp.bfloat16)
    return jnp.dot(hidden, down_w, preferred_element_type=jnp.float32).astype(jnp.bfloat16)


def gather(held):
    return lax.all_gather(held, "sc", axis=0, tiled=True)


def expert_parts(gathered, slices):
    chips = lax.axis_size("sc")
    count = gathered.shape[0] // chips
    width = gathered.shape[1]
    total = None
    for gate_w, up_w, down_w in slices:
        part = slice_ffn(gathered, gate_w, up_w, down_w).astype(jnp.float32)
        total = part if total is None else total + part
    return total.astype(jnp.bfloat16).reshape(chips, count, width)


def chip_sums(paired):
    return lax.all_to_all(paired, "sc", split_axis=0, concat_axis=0, tiled=True)


def finish(back, weights):
    summed = jnp.sum(back.astype(jnp.float32), axis=0)
    return (summed * weights[:, None]).astype(jnp.bfloat16)


def shards(tokens, parents, expert_ids, route_weights, w_gate, w_up, w_down):
    count, width = tokens.shape
    picks_row = expert_ids.shape[1]
    experts = lax.axis_size("eg")
    group = lax.axis_index("eg")
    slots = 5 * count * picks_row // (4 * experts)
    nodes = jnp.arange(count, dtype=jnp.int32)
    parent_hot = (parents[:, None] == nodes[None, :]).astype(jnp.bfloat16)
    lifted = tokens.astype(jnp.float32) + jnp.dot(
        parent_hot, tokens, preferred_element_type=jnp.float32
    )
    normed = (lifted * lax.rsqrt(jnp.mean(lifted * lifted, axis=1, keepdims=True) + 1e-06)).astype(
        jnp.bfloat16
    )
    relative = (expert_ids - group) % experts
    picks = relative[:, :, None] == jnp.arange(experts, dtype=jnp.int32)[None, None, :]
    chosen = jnp.any(picks, axis=1).astype(jnp.int32)
    before = jnp.cumsum(chosen, axis=0) - chosen
    slot_iota = jnp.arange(slots, dtype=jnp.int32)
    place = (chosen[:, :, None] * (before[:, :, None] == slot_iota[None, None, :])) > 0
    weight_te = jnp.sum(jnp.where(picks, route_weights[:, :, None], 0.0), axis=1)
    packed = jnp.einsum(
        "tkc,td->kcd", place.astype(jnp.bfloat16), normed, preferred_element_type=jnp.float32
    ).astype(jnp.bfloat16)
    packed_w = jnp.sum(jnp.where(place, weight_te[:, :, None], 0.0), axis=0)
    cores = lax.axis_size("core")
    swap = [(c, (c + 1) % cores) for c in range(cores)]
    mine = (w_gate[0], w_up[0], w_down[0])
    weights = (mine, tuple(lax.ppermute(w, "core", swap) for w in mine))

    def shift(k):
        return [(g, (g + k) % experts) for g in range(experts)]

    away = [lax.ppermute(packed[k], "eg", shift(k)) for k in range(1, experts)]
    away_w = [lax.ppermute(packed_w[k], "eg", shift(k)) for k in range(1, experts)]
    own_rows = gather(packed[0])
    own_rows, away, away_w = lax.optimization_barrier((own_rows, away, away_w))
    own_parts = expert_parts(own_rows, weights)
    away_rows = gather(jnp.concatenate(away, axis=0))
    own_parts, away_rows = lax.optimization_barrier((own_parts, away_rows))
    away_parts = expert_parts(away_rows, weights)
    away_back = chip_sums(away_parts)
    own_parts, away_back = lax.optimization_barrier((own_parts, away_back))
    done = finish(away_back, jnp.concatenate(away_w, axis=0))
    own = finish(chip_sums(own_parts), packed_w[0])
    home = [own] + [
        lax.ppermute(done[(k - 1) * slots:k * slots], "eg", shift(experts - k))
        for k in range(1, experts)
    ]
    result = jnp.einsum(
        "tkc,kcd->td",
        place.astype(jnp.bfloat16),
        jnp.stack(home),
        preferred_element_type=jnp.float32,
    )
    return result.astype(jnp.bfloat16)


def solution(mesh):
    groups, ranks = mesh.devices.shape
    experts = ranks // SLICES
    cores = 2
    split = Mesh(
        mesh.devices.reshape(groups, experts, SLICES // cores, cores), ("grp", "eg", "sc", "core")
    )
    rows = ("grp", "eg", "sc", "core")
    placed = (
        P(rows, None),
        P(rows),
        P(rows, None),
        P(rows, None),
        P(("eg", "sc", "core"), None, None),
        P(("eg", "sc", "core"), None, None),
        P(("eg", "sc", "core"), None, None),
    )
    return jax.shard_map(
        shards, mesh=split, in_specs=placed, out_specs=P(rows, None), check_vma=False
    )
```

```python
import jax
import jax.numpy as jnp
from jax import lax
from jax.sharding import Mesh
from jax.sharding import PartitionSpec as P

SLICES = 8


def slice_ffn(rows, gate_w, up_w, down_w):
    gate = jnp.dot(rows, gate_w, preferred_element_type=jnp.float32)
    upper = jnp.dot(rows, up_w, preferred_element_type=jnp.float32)
    hidden = (jax.nn.silu(gate) * upper).astype(jnp.bfloat16)
    return jnp.dot(hidden, down_w, preferred_element_type=jnp.float32).astype(jnp.bfloat16)


def gather(held):
    return lax.all_gather(held, ("core", "sc"), axis=0, tiled=True)


def expert_parts(gathered, gate_w, up_w, down_w):
    chips = lax.axis_size("sc")
    cores = lax.axis_size("core")
    count = gathered.shape[0] // (chips * cores)
    width = gathered.shape[1]
    halves = gathered.reshape(cores, chips * count, width)
    core = lax.axis_index("core")
    swap = [(c, (c + 1) % cores) for c in range(cores)]
    sent = slice_ffn(halves[(core + 1) % cores], gate_w, up_w, down_w)
    sibling = lax.ppermute(sent, "core", swap)
    kept = slice_ffn(halves[core], gate_w, up_w, down_w)
    paired = (kept.astype(jnp.float32) + sibling.astype(jnp.float32)).astype(jnp.bfloat16)
    return paired.reshape(chips, count, width)


def chip_sums(paired):
    return lax.all_to_all(paired, "sc", split_axis=0, concat_axis=0, tiled=True)


def finish(back, weights):
    summed = jnp.sum(back.astype(jnp.float32), axis=0)
    return (summed * weights[:, None]).astype(jnp.bfloat16)


def shards(tokens, parents, expert_ids, route_weights, w_gate, w_up, w_down):
    count, width = tokens.shape
    picks_row = expert_ids.shape[1]
    experts = lax.axis_size("eg")
    group = lax.axis_index("eg")
    slots = 5 * count * picks_row // (4 * experts)
    nodes = jnp.arange(count, dtype=jnp.int32)
    parent_hot = (parents[:, None] == nodes[None, :]).astype(jnp.bfloat16)
    lifted = tokens.astype(jnp.float32) + jnp.dot(
        parent_hot, tokens, preferred_element_type=jnp.float32
    )
    normed = (lifted * lax.rsqrt(jnp.mean(lifted * lifted, axis=1, keepdims=True) + 1e-06)).astype(
        jnp.bfloat16
    )
    relative = (expert_ids - group) % experts
    picks = relative[:, :, None] == jnp.arange(experts, dtype=jnp.int32)[None, None, :]
    chosen = jnp.any(picks, axis=1).astype(jnp.int32)
    before = jnp.cumsum(chosen, axis=0) - chosen
    slot_iota = jnp.arange(slots, dtype=jnp.int32)
    place = (chosen[:, :, None] * (before[:, :, None] == slot_iota[None, None, :])) > 0
    weight_te = jnp.sum(jnp.where(picks, route_weights[:, :, None], 0.0), axis=1)
    packed = jnp.einsum(
        "tkc,td->kcd", place.astype(jnp.bfloat16), normed, preferred_element_type=jnp.float32
    ).astype(jnp.bfloat16)
    packed_w = jnp.sum(jnp.where(place, weight_te[:, :, None], 0.0), axis=0)
    weights = (w_gate[0], w_up[0], w_down[0])

    def shift(k):
        return [(g, (g + k) % experts) for g in range(experts)]

    away = [lax.ppermute(packed[k], "eg", shift(k)) for k in range(1, experts)]
    away_w = [lax.ppermute(packed_w[k], "eg", shift(k)) for k in range(1, experts)]
    own_rows = gather(packed[0])
    own_rows, away, away_w = lax.optimization_barrier((own_rows, away, away_w))
    own_parts = expert_parts(own_rows, *weights)
    away_rows = gather(jnp.concatenate(away, axis=0))
    own_parts, away_rows = lax.optimization_barrier((own_parts, away_rows))
    away_parts = expert_parts(away_rows, *weights)
    away_back = chip_sums(away_parts)
    own_parts, away_back = lax.optimization_barrier((own_parts, away_back))
    done = finish(away_back, jnp.concatenate(away_w, axis=0))
    own = finish(chip_sums(own_parts), packed_w[0])
    home = [own] + [
        lax.ppermute(done[(k - 1) * slots:k * slots], "eg", shift(experts - k))
        for k in range(1, experts)
    ]
    result = jnp.einsum(
        "tkc,kcd->td",
        place.astype(jnp.bfloat16),
        jnp.stack(home),
        preferred_element_type=jnp.float32,
    )
    return result.astype(jnp.bfloat16)


def solution(mesh):
    groups, ranks = mesh.devices.shape
    experts = ranks // SLICES
    cores = 2
    split = Mesh(
        mesh.devices.reshape(groups, experts, SLICES // cores, cores), ("grp", "eg", "sc", "core")
    )
    rows = ("grp", "eg", "sc", "core")
    placed = (
        P(rows, None),
        P(rows),
        P(rows, None),
        P(rows, None),
        P(("eg", "sc", "core"), None, None),
        P(("eg", "sc", "core"), None, None),
        P(("eg", "sc", "core"), None, None),
    )
    return jax.shard_map(
        shards, mesh=split, in_specs=placed, out_specs=P(rows, None), check_vma=False
    )
```

```python
import jax
import jax.numpy as jnp
from jax import lax
from jax.sharding import Mesh
from jax.sharding import PartitionSpec as P

SLICES = 8


def slice_ffn(rows, gate_up_w, down_w):
    both = jnp.dot(rows, gate_up_w, preferred_element_type=jnp.float32)
    gate, upper = jnp.split(both, 2, axis=1)
    hidden = (jax.nn.silu(gate) * upper).astype(jnp.bfloat16)
    return jnp.dot(hidden, down_w, preferred_element_type=jnp.float32).astype(jnp.bfloat16)


def gather(held):
    return lax.all_gather(held, ("core", "sc"), axis=0, tiled=True)


def expert_parts(gathered, gate_up_w, down_w):
    chips = lax.axis_size("sc")
    cores = lax.axis_size("core")
    count = gathered.shape[0] // (chips * cores)
    width = gathered.shape[1]
    parts = slice_ffn(gathered, gate_up_w, down_w)
    halves = parts.reshape(cores, chips * count, width)
    core = lax.axis_index("core")
    swap = [(c, (c + 1) % cores) for c in range(cores)]
    sibling = lax.ppermute(halves[(core + 1) % cores], "core", swap)
    paired = (halves[core].astype(jnp.float32) + sibling.astype(jnp.float32)).astype(jnp.bfloat16)
    return paired.reshape(chips, count, width)


def chip_sums(paired):
    return lax.all_to_all(paired, "sc", split_axis=0, concat_axis=0, tiled=True)


def finish(back, weights):
    summed = jnp.sum(back.astype(jnp.float32), axis=0)
    return (summed * weights[:, None]).astype(jnp.bfloat16)


def shards(tokens, parents, expert_ids, route_weights, w_gate, w_up, w_down):
    count, width = tokens.shape
    picks_row = expert_ids.shape[1]
    experts = lax.axis_size("eg")
    group = lax.axis_index("eg")
    slots = 5 * count * picks_row // (4 * experts)
    nodes = jnp.arange(count, dtype=jnp.int32)
    parent_hot = (parents[:, None] == nodes[None, :]).astype(jnp.bfloat16)
    lifted = tokens.astype(jnp.float32) + jnp.dot(
        parent_hot, tokens, preferred_element_type=jnp.float32
    )
    normed = (lifted * lax.rsqrt(jnp.mean(lifted * lifted, axis=1, keepdims=True) + 1e-06)).astype(
        jnp.bfloat16
    )
    relative = (expert_ids - group) % experts
    picks = relative[:, :, None] == jnp.arange(experts, dtype=jnp.int32)[None, None, :]
    chosen = jnp.any(picks, axis=1).astype(jnp.int32)
    before = jnp.cumsum(chosen, axis=0) - chosen
    slot_iota = jnp.arange(slots, dtype=jnp.int32)
    place = (chosen[:, :, None] * (before[:, :, None] == slot_iota[None, None, :])) > 0
    weight_te = jnp.sum(jnp.where(picks, route_weights[:, :, None], 0.0), axis=1)
    packed = jnp.einsum(
        "tkc,td->kcd", place.astype(jnp.bfloat16), normed, preferred_element_type=jnp.float32
    ).astype(jnp.bfloat16)
    packed_w = jnp.sum(jnp.where(place, weight_te[:, :, None], 0.0), axis=0)
    weights = (jnp.concatenate([w_gate[0], w_up[0]], axis=1), w_down[0])

    def shift(k):
        return [(g, (g + k) % experts) for g in range(experts)]

    away = [lax.ppermute(packed[k], "eg", shift(k)) for k in range(1, experts)]
    away_w = [lax.ppermute(packed_w[k], "eg", shift(k)) for k in range(1, experts)]
    own_rows = gather(packed[0])
    own_rows, away, away_w = lax.optimization_barrier((own_rows, away, away_w))
    own_parts = expert_parts(own_rows, *weights)
    away_rows = gather(jnp.concatenate(away, axis=0))
    own_parts, away_rows = lax.optimization_barrier((own_parts, away_rows))
    away_parts = expert_parts(away_rows, *weights)
    away_back = chip_sums(away_parts)
    own_parts, away_back = lax.optimization_barrier((own_parts, away_back))
    done = finish(away_back, jnp.concatenate(away_w, axis=0))
    own = finish(chip_sums(own_parts), packed_w[0])
    home = [own] + [
        lax.ppermute(done[(k - 1) * slots:k * slots], "eg", shift(experts - k))
        for k in range(1, experts)
    ]
    result = jnp.einsum(
        "tkc,kcd->td",
        place.astype(jnp.bfloat16),
        jnp.stack(home),
        preferred_element_type=jnp.float32,
    )
    return result.astype(jnp.bfloat16)


def solution(mesh):
    groups, ranks = mesh.devices.shape
    experts = ranks // SLICES
    cores = 2
    split = Mesh(
        mesh.devices.reshape(groups, experts, SLICES // cores, cores), ("grp", "eg", "sc", "core")
    )
    rows = ("grp", "eg", "sc", "core")
    placed = (
        P(rows, None),
        P(rows),
        P(rows, None),
        P(rows, None),
        P(("eg", "sc", "core"), None, None),
        P(("eg", "sc", "core"), None, None),
        P(("eg", "sc", "core"), None, None),
    )
    return jax.shard_map(
        shards, mesh=split, in_specs=placed, out_specs=P(rows, None), check_vma=False
    )
```

```python
import jax
import jax.numpy as jnp
from jax import lax
from jax.sharding import Mesh
from jax.sharding import PartitionSpec as P

SLICES = 8


def slice_ffn(rows, gate_up_w, down_w):
    both = jnp.dot(rows, gate_up_w, preferred_element_type=jnp.float32)
    gate, upper = jnp.split(both, 2, axis=1)
    hidden = (jax.nn.silu(gate) * upper).astype(jnp.bfloat16)
    return jnp.dot(hidden, down_w, preferred_element_type=jnp.float32).astype(jnp.bfloat16)


def gather(held):
    return lax.all_gather(held, ("core", "sc"), axis=0, tiled=True)


def expert_parts(gathered, gate_up_w, down_w):
    chips = lax.axis_size("sc")
    cores = lax.axis_size("core")
    count = gathered.shape[0] // (chips * cores)
    width = gathered.shape[1]
    parts = slice_ffn(gathered, gate_up_w, down_w)
    halves = parts.reshape(cores, chips * count, width)
    core = lax.axis_index("core")
    swap = [(c, (c + 1) % cores) for c in range(cores)]
    sibling = lax.ppermute(halves[(core + 1) % cores], "core", swap)
    paired = (halves[core].astype(jnp.float32) + sibling.astype(jnp.float32)).astype(jnp.bfloat16)
    return paired.reshape(chips, count, width)


def gather_by_core(held):
    chips = lax.axis_size("sc")
    cores = lax.axis_size("core")
    swap = [(c, (c + 1) % cores) for c in range(cores)]
    spread = jnp.broadcast_to(held[None], (chips,) + held.shape)
    mine = lax.all_to_all(spread, "sc", split_axis=0, concat_axis=0, tiled=True)
    return mine, lax.ppermute(mine, "core", swap)


def expert_parts_by_core(rows, gate_up_w, down_w):
    mine, theirs = rows
    cores = lax.axis_size("core")
    swap = [(c, (c + 1) % cores) for c in range(cores)]
    chips, count, width = mine.shape
    parts = slice_ffn(
        jnp.concatenate([theirs, mine], axis=0).reshape(2 * chips * count, width), gate_up_w, down_w
    )
    sibling = lax.ppermute(parts[:chips * count], "core", swap)
    kept = parts[chips * count:]
    paired = (kept.astype(jnp.float32) + sibling.astype(jnp.float32)).astype(jnp.bfloat16)
    return paired.reshape(chips, count, width)


def chip_sums(paired):
    return lax.all_to_all(paired, "sc", split_axis=0, concat_axis=0, tiled=True)


def finish(back, weights):
    summed = jnp.sum(back.astype(jnp.float32), axis=0)
    return (summed * weights[:, None]).astype(jnp.bfloat16)


def shards(tokens, parents, expert_ids, route_weights, w_gate, w_up, w_down):
    count, width = tokens.shape
    picks_row = expert_ids.shape[1]
    experts = lax.axis_size("eg")
    group = lax.axis_index("eg")
    slots = 5 * count * picks_row // (4 * experts)
    nodes = jnp.arange(count, dtype=jnp.int32)
    parent_hot = (parents[:, None] == nodes[None, :]).astype(jnp.bfloat16)
    lifted = tokens.astype(jnp.float32) + jnp.dot(
        parent_hot, tokens, preferred_element_type=jnp.float32
    )
    normed = (lifted * lax.rsqrt(jnp.mean(lifted * lifted, axis=1, keepdims=True) + 1e-06)).astype(
        jnp.bfloat16
    )
    relative = (expert_ids - group) % experts
    picks = relative[:, :, None] == jnp.arange(experts, dtype=jnp.int32)[None, None, :]
    chosen = jnp.any(picks, axis=1).astype(jnp.int32)
    before = jnp.cumsum(chosen, axis=0) - chosen
    slot_iota = jnp.arange(slots, dtype=jnp.int32)
    place = (chosen[:, :, None] * (before[:, :, None] == slot_iota[None, None, :])) > 0
    weight_te = jnp.sum(jnp.where(picks, route_weights[:, :, None], 0.0), axis=1)
    packed = jnp.einsum(
        "tkc,td->kcd", place.astype(jnp.bfloat16), normed, preferred_element_type=jnp.float32
    ).astype(jnp.bfloat16)
    packed_w = jnp.sum(jnp.where(place, weight_te[:, :, None], 0.0), axis=0)
    weights = (jnp.concatenate([w_gate[0], w_up[0]], axis=1), w_down[0])

    def shift(k):
        return [(g, (g + k) % experts) for g in range(experts)]

    away = [lax.ppermute(packed[k], "eg", shift(k)) for k in range(1, experts)]
    away_w = [lax.ppermute(packed_w[k], "eg", shift(k)) for k in range(1, experts)]
    own_rows = gather(packed[0])
    away, away_w = lax.optimization_barrier((away, away_w))
    own_parts = expert_parts(own_rows, *weights)
    away_rows = gather_by_core(jnp.concatenate(away, axis=0))
    own_parts, away_rows = lax.optimization_barrier((own_parts, away_rows))
    away_parts = expert_parts_by_core(away_rows, *weights)
    away_back = chip_sums(away_parts)
    own_parts, away_back = lax.optimization_barrier((own_parts, away_back))
    done = finish(away_back, jnp.concatenate(away_w, axis=0))
    own = finish(chip_sums(own_parts), packed_w[0])
    home = [own] + [
        lax.ppermute(done[(k - 1) * slots:k * slots], "eg", shift(experts - k))
        for k in range(1, experts)
    ]
    result = jnp.einsum(
        "tkc,kcd->td",
        place.astype(jnp.bfloat16),
        jnp.stack(home),
        preferred_element_type=jnp.float32,
    )
    return result.astype(jnp.bfloat16)


def solution(mesh):
    groups, ranks = mesh.devices.shape
    experts = ranks // SLICES
    cores = 2
    split = Mesh(
        mesh.devices.reshape(groups, experts, SLICES // cores, cores), ("grp", "eg", "sc", "core")
    )
    rows = ("grp", "eg", "sc", "core")
    placed = (
        P(rows, None),
        P(rows),
        P(rows, None),
        P(rows, None),
        P(("eg", "sc", "core"), None, None),
        P(("eg", "sc", "core"), None, None),
        P(("eg", "sc", "core"), None, None),
    )
    return jax.shard_map(
        shards, mesh=split, in_specs=placed, out_specs=P(rows, None), check_vma=False
    )
```

```python
import jax
import jax.numpy as jnp
from jax import lax
from jax.sharding import Mesh
from jax.sharding import PartitionSpec as P

SLICES = 8


def slice_ffn(rows, gate_up_w, down_w):
    both = jnp.dot(rows, gate_up_w, preferred_element_type=jnp.float32)
    gate, upper = jnp.split(both, 2, axis=1)
    hidden = (jax.nn.silu(gate) * upper).astype(jnp.bfloat16)
    return jnp.dot(hidden, down_w, preferred_element_type=jnp.float32).astype(jnp.bfloat16)


def gather(held):
    return lax.all_gather(held, ("core", "sc"), axis=0, tiled=True)


def expert_parts(gathered, gate_up_w, down_w):
    chips = lax.axis_size("sc")
    cores = lax.axis_size("core")
    count = gathered.shape[0] // (chips * cores)
    width = gathered.shape[1]
    parts = slice_ffn(gathered, gate_up_w, down_w)
    halves = parts.reshape(cores, chips * count, width)
    core = lax.axis_index("core")
    swap = [(c, (c + 1) % cores) for c in range(cores)]
    sibling = lax.ppermute(halves[(core + 1) % cores], "core", swap)
    paired = (halves[core].astype(jnp.float32) + sibling.astype(jnp.float32)).astype(jnp.bfloat16)
    return paired.reshape(chips, count, width)


def chip_sums(paired):
    return lax.all_to_all(paired, "sc", split_axis=0, concat_axis=0, tiled=True)


def finish(back, weights):
    summed = jnp.sum(back.astype(jnp.float32), axis=0)
    return (summed * weights[:, None]).astype(jnp.bfloat16)


def shards(tokens, parents, expert_ids, route_weights, w_gate, w_up, w_down):
    count, width = tokens.shape
    picks_row = expert_ids.shape[1]
    experts = lax.axis_size("eg")
    group = lax.axis_index("eg")
    slots = 5 * count * picks_row // (4 * experts)
    nodes = jnp.arange(count, dtype=jnp.int32)
    parent_hot = (parents[:, None] == nodes[None, :]).astype(jnp.bfloat16)
    lifted = tokens.astype(jnp.float32) + jnp.dot(
        parent_hot, tokens, preferred_element_type=jnp.float32
    )
    normed = (lifted * lax.rsqrt(jnp.mean(lifted * lifted, axis=1, keepdims=True) + 1e-06)).astype(
        jnp.bfloat16
    )
    relative = (expert_ids - group) % experts
    picks = relative[:, :, None] == jnp.arange(experts, dtype=jnp.int32)[None, None, :]
    chosen = jnp.any(picks, axis=1).astype(jnp.int32)
    before = jnp.cumsum(chosen, axis=0) - chosen
    slot_iota = jnp.arange(slots, dtype=jnp.int32)
    place = (chosen[:, :, None] * (before[:, :, None] == slot_iota[None, None, :])) > 0
    weight_te = jnp.sum(jnp.where(picks, route_weights[:, :, None], 0.0), axis=1)
    packed = jnp.einsum(
        "tkc,td->kcd", place.astype(jnp.bfloat16), normed, preferred_element_type=jnp.float32
    ).astype(jnp.bfloat16)
    packed_w = jnp.sum(jnp.where(place, weight_te[:, :, None], 0.0), axis=0)
    weights = (jnp.concatenate([w_gate[0], w_up[0]], axis=1), w_down[0])

    def shift(k):
        return [(g, (g + k) % experts) for g in range(experts)]

    away = [lax.ppermute(packed[k], "eg", shift(k)) for k in range(1, experts)]
    away_w = [lax.ppermute(packed_w[k], "eg", shift(k)) for k in range(1, experts)]
    own_rows = gather(packed[0])
    own_rows, away, away_w = lax.optimization_barrier((own_rows, away, away_w))
    own_parts = expert_parts(own_rows, *weights)
    away_rows = gather(jnp.concatenate(away, axis=0))
    own_parts, away_rows = lax.optimization_barrier((own_parts, away_rows))
    away_parts = expert_parts(away_rows, *weights)
    away_back = chip_sums(away_parts)
    done = finish(away_back, jnp.concatenate(away_w, axis=0))
    own_parts, done = lax.optimization_barrier((own_parts, done))
    own = finish(chip_sums(own_parts), packed_w[0])
    home = [own] + [
        lax.ppermute(done[(k - 1) * slots:k * slots], "eg", shift(experts - k))
        for k in range(1, experts)
    ]
    result = jnp.einsum(
        "tkc,kcd->td",
        place.astype(jnp.bfloat16),
        jnp.stack(home),
        preferred_element_type=jnp.float32,
    )
    return result.astype(jnp.bfloat16)


def solution(mesh):
    groups, ranks = mesh.devices.shape
    experts = ranks // SLICES
    cores = 2
    split = Mesh(
        mesh.devices.reshape(groups, experts, SLICES // cores, cores), ("grp", "eg", "sc", "core")
    )
    rows = ("grp", "eg", "sc", "core")
    placed = (
        P(rows, None),
        P(rows),
        P(rows, None),
        P(rows, None),
        P(("eg", "sc", "core"), None, None),
        P(("eg", "sc", "core"), None, None),
        P(("eg", "sc", "core"), None, None),
    )
    return jax.shard_map(
        shards, mesh=split, in_specs=placed, out_specs=P(rows, None), check_vma=False
    )
```

```python
import jax
import jax.numpy as jnp
from jax import lax
from jax.sharding import Mesh
from jax.sharding import PartitionSpec as P

SLICES = 8


def slice_ffn(rows, gate_up_w, down_w):
    both = jnp.dot(rows, gate_up_w, preferred_element_type=jnp.float32)
    gate, upper = jnp.split(both, 2, axis=1)
    hidden = (jax.nn.silu(gate) * upper).astype(jnp.bfloat16)
    return jnp.dot(hidden, down_w, preferred_element_type=jnp.float32).astype(jnp.bfloat16)


def gather(held):
    return lax.all_gather(held, ("core", "sc"), axis=0, tiled=True)


def expert_parts(gathered, gate_up_w, down_w):
    chips = lax.axis_size("sc")
    cores = lax.axis_size("core")
    count = gathered.shape[0] // (chips * cores)
    width = gathered.shape[1]
    parts = slice_ffn(gathered, gate_up_w, down_w)
    halves = parts.reshape(cores, chips * count, width)
    core = lax.axis_index("core")
    swap = [(c, (c + 1) % cores) for c in range(cores)]
    sibling = lax.ppermute(halves[(core + 1) % cores], "core", swap)
    paired = (halves[core].astype(jnp.float32) + sibling.astype(jnp.float32)).astype(jnp.bfloat16)
    return paired.reshape(chips, count, width)


def chip_sums(paired):
    return lax.all_to_all(paired, "sc", split_axis=0, concat_axis=0, tiled=True)


def finish(back, weights):
    summed = jnp.sum(back.astype(jnp.float32), axis=0)
    return (summed * weights[:, None]).astype(jnp.bfloat16)


def shards(tokens, parents, expert_ids, route_weights, w_gate, w_up, w_down):
    count, width = tokens.shape
    picks_row = expert_ids.shape[1]
    experts = lax.axis_size("eg")
    group = lax.axis_index("eg")
    slots = 5 * count * picks_row // (4 * experts)
    nodes = jnp.arange(count, dtype=jnp.int32)
    parent_hot = (parents[:, None] == nodes[None, :]).astype(jnp.bfloat16)
    lifted = tokens.astype(jnp.float32) + jnp.dot(
        parent_hot, tokens, preferred_element_type=jnp.float32
    )
    normed = (lifted * lax.rsqrt(jnp.mean(lifted * lifted, axis=1, keepdims=True) + 1e-06)).astype(
        jnp.bfloat16
    )
    relative = (expert_ids - group) % experts
    picks = relative[:, :, None] == jnp.arange(experts, dtype=jnp.int32)[None, None, :]
    chosen = jnp.any(picks, axis=1).astype(jnp.int32)
    before = jnp.cumsum(chosen, axis=0) - chosen
    slot_iota = jnp.arange(slots, dtype=jnp.int32)
    place = (chosen[:, :, None] * (before[:, :, None] == slot_iota[None, None, :])) > 0
    weight_te = jnp.sum(jnp.where(picks, route_weights[:, :, None], 0.0), axis=1)
    packed = jnp.einsum(
        "tkc,td->kcd", place.astype(jnp.bfloat16), normed, preferred_element_type=jnp.float32
    ).astype(jnp.bfloat16)
    packed_w = jnp.sum(jnp.where(place, weight_te[:, :, None], 0.0), axis=0)
    weights = (jnp.concatenate([w_gate[0], w_up[0]], axis=1), w_down[0])

    def shift(k):
        return [(g, (g + k) % experts) for g in range(experts)]

    away = [lax.ppermute(packed[k], "eg", shift(k)) for k in range(1, experts)]
    away_w = [lax.ppermute(packed_w[k], "eg", shift(k)) for k in range(1, experts)]
    early = slots * 3 // 5
    own_rows = gather(packed[0][:early])
    own_rows, away, away_w = lax.optimization_barrier((own_rows, away, away_w))
    own_parts = expert_parts(own_rows, *weights)
    late_rows = jnp.concatenate(away + [packed[0][early:]], axis=0)
    late_w = jnp.concatenate(away_w + [packed_w[0][early:]], axis=0)
    away_rows = gather(late_rows)
    own_parts, away_rows = lax.optimization_barrier((own_parts, away_rows))
    away_parts = expert_parts(away_rows, *weights)
    away_back = chip_sums(away_parts)
    late = finish(away_back, late_w)
    done = late[:(experts - 1) * slots]
    own_parts, done = lax.optimization_barrier((own_parts, done))
    own = jnp.concatenate(
        [finish(chip_sums(own_parts), packed_w[0][:early]), late[(experts - 1) * slots:]], axis=0
    )
    home = [own] + [
        lax.ppermute(done[(k - 1) * slots:k * slots], "eg", shift(experts - k))
        for k in range(1, experts)
    ]
    result = jnp.einsum(
        "tkc,kcd->td",
        place.astype(jnp.bfloat16),
        jnp.stack(home),
        preferred_element_type=jnp.float32,
    )
    return result.astype(jnp.bfloat16)


def solution(mesh):
    groups, ranks = mesh.devices.shape
    experts = ranks // SLICES
    cores = 2
    split = Mesh(
        mesh.devices.reshape(groups, experts, SLICES // cores, cores), ("grp", "eg", "sc", "core")
    )
    rows = ("grp", "eg", "sc", "core")
    placed = (
        P(rows, None),
        P(rows),
        P(rows, None),
        P(rows, None),
        P(("eg", "sc", "core"), None, None),
        P(("eg", "sc", "core"), None, None),
        P(("eg", "sc", "core"), None, None),
    )
    return jax.shard_map(
        shards, mesh=split, in_specs=placed, out_specs=P(rows, None), check_vma=False
    )
```

```python
import jax
import jax.numpy as jnp
from jax import lax
from jax.sharding import Mesh
from jax.sharding import PartitionSpec as P

SLICES = 8


def slice_ffn(rows, gate_up_w, down_w):
    both = jnp.dot(rows, gate_up_w, preferred_element_type=jnp.float32)
    gate, upper = jnp.split(both, 2, axis=1)
    hidden = (jax.nn.silu(gate) * upper).astype(jnp.bfloat16)
    return jnp.dot(hidden, down_w, preferred_element_type=jnp.float32).astype(jnp.bfloat16)


def gather(held):
    return lax.all_gather(held, ("core", "sc"), axis=0, tiled=True)


def expert_parts(gathered, gate_up_w, down_w):
    chips = lax.axis_size("sc")
    cores = lax.axis_size("core")
    count = gathered.shape[0] // (chips * cores)
    width = gathered.shape[1]
    parts = slice_ffn(gathered, gate_up_w, down_w)
    halves = parts.reshape(cores, chips * count, width)
    core = lax.axis_index("core")
    swap = [(c, (c + 1) % cores) for c in range(cores)]
    sibling = lax.ppermute(halves[(core + 1) % cores], "core", swap)
    paired = (halves[core].astype(jnp.float32) + sibling.astype(jnp.float32)).astype(jnp.bfloat16)
    return paired.reshape(chips, count, width)


def chip_sums(paired):
    return lax.all_to_all(paired, "sc", split_axis=0, concat_axis=0, tiled=True)


def finish(back, weights):
    summed = jnp.sum(back.astype(jnp.float32), axis=0)
    return (summed * weights[:, None]).astype(jnp.bfloat16)


def shards(tokens, parents, expert_ids, route_weights, w_gate, w_up, w_down):
    count, width = tokens.shape
    picks_row = expert_ids.shape[1]
    experts = lax.axis_size("eg")
    group = lax.axis_index("eg")
    slots = 5 * count * picks_row // (4 * experts)
    nodes = jnp.arange(count, dtype=jnp.int32)
    parent_hot = (parents[:, None] == nodes[None, :]).astype(jnp.bfloat16)
    lifted = tokens.astype(jnp.float32) + jnp.dot(
        parent_hot, tokens, preferred_element_type=jnp.float32
    )
    normed = (lifted * lax.rsqrt(jnp.mean(lifted * lifted, axis=1, keepdims=True) + 1e-06)).astype(
        jnp.bfloat16
    )
    relative = (expert_ids - group) % experts
    picks = relative[:, :, None] == jnp.arange(experts, dtype=jnp.int32)[None, None, :]
    chosen = jnp.any(picks, axis=1).astype(jnp.int32)
    before = jnp.cumsum(chosen, axis=0) - chosen
    slot_iota = jnp.arange(slots, dtype=jnp.int32)
    place = (chosen[:, :, None] * (before[:, :, None] == slot_iota[None, None, :])) > 0
    weight_te = jnp.sum(jnp.where(picks, route_weights[:, :, None], 0.0), axis=1)
    packed = jnp.einsum(
        "tkc,td->kcd", place.astype(jnp.bfloat16), normed, preferred_element_type=jnp.float32
    ).astype(jnp.bfloat16)
    packed_w = jnp.sum(jnp.where(place, weight_te[:, :, None], 0.0), axis=0)
    weights = (jnp.concatenate([w_gate[0], w_up[0]], axis=1), w_down[0])

    def shift(k):
        return [(g, (g + k) % experts) for g in range(experts)]

    half = slots // 2

    def cross(rows, k):
        return jnp.concatenate(
            [lax.ppermute(rows[:half], "eg", shift(k)), lax.ppermute(rows[half:], "eg", shift(k))]
        )

    away = [cross(packed[k], k) for k in range(1, experts)]
    away_w = [lax.ppermute(packed_w[k], "eg", shift(k)) for k in range(1, experts)]
    own_rows = gather(packed[0])
    own_rows, away, away_w = lax.optimization_barrier((own_rows, away, away_w))
    own_parts = expert_parts(own_rows, *weights)
    away_rows = gather(jnp.concatenate(away, axis=0))
    own_parts, away_rows = lax.optimization_barrier((own_parts, away_rows))
    away_parts = expert_parts(away_rows, *weights)
    away_back = chip_sums(away_parts)
    done = finish(away_back, jnp.concatenate(away_w, axis=0))
    own_parts, done = lax.optimization_barrier((own_parts, done))
    own = finish(chip_sums(own_parts), packed_w[0])
    home = [own] + [
        cross(done[(k - 1) * slots:k * slots], experts - k)
        for k in range(1, experts)
    ]
    result = jnp.einsum(
        "tkc,kcd->td",
        place.astype(jnp.bfloat16),
        jnp.stack(home),
        preferred_element_type=jnp.float32,
    )
    return result.astype(jnp.bfloat16)


def solution(mesh):
    groups, ranks = mesh.devices.shape
    experts = ranks // SLICES
    cores = 2
    split = Mesh(
        mesh.devices.reshape(groups, experts, SLICES // cores, cores), ("grp", "eg", "sc", "core")
    )
    rows = ("grp", "eg", "sc", "core")
    placed = (
        P(rows, None),
        P(rows),
        P(rows, None),
        P(rows, None),
        P(("eg", "sc", "core"), None, None),
        P(("eg", "sc", "core"), None, None),
        P(("eg", "sc", "core"), None, None),
    )
    return jax.shard_map(
        shards, mesh=split, in_specs=placed, out_specs=P(rows, None), check_vma=False
    )
```

```python
import jax
import jax.numpy as jnp
from jax import lax
from jax.sharding import Mesh
from jax.sharding import PartitionSpec as P

SLICES = 8


def slice_ffn(rows, gate_up_w, down_w):
    both = jnp.dot(rows, gate_up_w, preferred_element_type=jnp.float32)
    gate, upper = jnp.split(both, 2, axis=1)
    hidden = (jax.nn.silu(gate) * upper).astype(jnp.bfloat16)
    return jnp.dot(hidden, down_w, preferred_element_type=jnp.float32).astype(jnp.bfloat16)


def gather(held):
    return lax.all_gather(held, ("core", "sc"), axis=0, tiled=True)


def expert_parts(gathered, gate_up_w, down_w):
    chips = lax.axis_size("sc")
    cores = lax.axis_size("core")
    count = gathered.shape[0] // (chips * cores)
    width = gathered.shape[1]
    parts = slice_ffn(gathered, gate_up_w, down_w)
    halves = parts.reshape(cores, chips * count, width)
    core = lax.axis_index("core")
    swap = [(c, (c + 1) % cores) for c in range(cores)]
    sibling = lax.ppermute(halves[(core + 1) % cores], "core", swap)
    paired = (halves[core].astype(jnp.float32) + sibling.astype(jnp.float32)).astype(jnp.bfloat16)
    return paired.reshape(chips, count, width)


def group_sums(parts):
    return lax.psum_scatter(parts, ("core", "sc"), scatter_dimension=0, tiled=True)


def chip_sums(paired):
    return lax.all_to_all(paired, "sc", split_axis=0, concat_axis=0, tiled=True)


def finish(back, weights):
    summed = jnp.sum(back.astype(jnp.float32), axis=0)
    return (summed * weights[:, None]).astype(jnp.bfloat16)


def shards(tokens, parents, expert_ids, route_weights, w_gate, w_up, w_down):
    count, width = tokens.shape
    picks_row = expert_ids.shape[1]
    experts = lax.axis_size("eg")
    group = lax.axis_index("eg")
    slots = 5 * count * picks_row // (4 * experts)
    nodes = jnp.arange(count, dtype=jnp.int32)
    parent_hot = (parents[:, None] == nodes[None, :]).astype(jnp.bfloat16)
    lifted = tokens.astype(jnp.float32) + jnp.dot(
        parent_hot, tokens, preferred_element_type=jnp.float32
    )
    normed = (lifted * lax.rsqrt(jnp.mean(lifted * lifted, axis=1, keepdims=True) + 1e-06)).astype(
        jnp.bfloat16
    )
    relative = (expert_ids - group) % experts
    picks = relative[:, :, None] == jnp.arange(experts, dtype=jnp.int32)[None, None, :]
    chosen = jnp.any(picks, axis=1).astype(jnp.int32)
    before = jnp.cumsum(chosen, axis=0) - chosen
    slot_iota = jnp.arange(slots, dtype=jnp.int32)
    place = (chosen[:, :, None] * (before[:, :, None] == slot_iota[None, None, :])) > 0
    weight_te = jnp.sum(jnp.where(picks, route_weights[:, :, None], 0.0), axis=1)
    packed = jnp.einsum(
        "tkc,td->kcd", place.astype(jnp.bfloat16), normed, preferred_element_type=jnp.float32
    ).astype(jnp.bfloat16)
    packed_w = jnp.sum(jnp.where(place, weight_te[:, :, None], 0.0), axis=0)
    weights = (jnp.concatenate([w_gate[0], w_up[0]], axis=1), w_down[0])

    def shift(k):
        return [(g, (g + k) % experts) for g in range(experts)]

    away = [lax.ppermute(packed[k], "eg", shift(k)) for k in range(1, experts)]
    away_w = [lax.ppermute(packed_w[k], "eg", shift(k)) for k in range(1, experts)]
    own_rows = gather(packed[0])
    own_rows, away, away_w = lax.optimization_barrier((own_rows, away, away_w))
    own_parts = slice_ffn(own_rows, *weights)
    away_rows = gather(jnp.concatenate(away, axis=0))
    own_parts, away_rows = lax.optimization_barrier((own_parts, away_rows))
    away_parts = expert_parts(away_rows, *weights)
    away_back = chip_sums(away_parts)
    own_sums = group_sums(own_parts)
    done = finish(away_back, jnp.concatenate(away_w, axis=0))
    own = finish(own_sums[None], packed_w[0])
    home = [own] + [
        lax.ppermute(done[(k - 1) * slots:k * slots], "eg", shift(experts - k))
        for k in range(1, experts)
    ]
    result = jnp.einsum(
        "tkc,kcd->td",
        place.astype(jnp.bfloat16),
        jnp.stack(home),
        preferred_element_type=jnp.float32,
    )
    return result.astype(jnp.bfloat16)


def solution(mesh):
    groups, ranks = mesh.devices.shape
    experts = ranks // SLICES
    cores = 2
    split = Mesh(
        mesh.devices.reshape(groups, experts, SLICES // cores, cores), ("grp", "eg", "sc", "core")
    )
    rows = ("grp", "eg", "sc", "core")
    placed = (
        P(rows, None),
        P(rows),
        P(rows, None),
        P(rows, None),
        P(("eg", "sc", "core"), None, None),
        P(("eg", "sc", "core"), None, None),
        P(("eg", "sc", "core"), None, None),
    )
    return jax.shard_map(
        shards, mesh=split, in_specs=placed, out_specs=P(rows, None), check_vma=False
    )
```

```python
import jax
import jax.numpy as jnp
from jax import lax
from jax.sharding import Mesh
from jax.sharding import PartitionSpec as P

SLICES = 8


def slice_ffn(rows, gate_w, up_w, down_w):
    gate = jnp.dot(rows, gate_w, preferred_element_type=jnp.float32)
    upper = jnp.dot(rows, up_w, preferred_element_type=jnp.float32)
    hidden = (jax.nn.silu(gate) * upper).astype(jnp.bfloat16)
    return jnp.dot(hidden, down_w, preferred_element_type=jnp.float32).astype(jnp.bfloat16)


def gather(held):
    return lax.all_gather(held, ("core", "sc"), axis=0, tiled=True)


def expert_parts(gathered, gate_w, up_w, down_w):
    chips = lax.axis_size("sc")
    cores = lax.axis_size("core")
    count = gathered.shape[0] // (chips * cores)
    width = gathered.shape[1]
    parts = slice_ffn(gathered, gate_w, up_w, down_w)
    halves = parts.reshape(cores, chips * count, width)
    core = lax.axis_index("core")
    swap = [(c, (c + 1) % cores) for c in range(cores)]
    sibling = lax.ppermute(halves[(core + 1) % cores], "core", swap)
    paired = (halves[core].astype(jnp.float32) + sibling.astype(jnp.float32)).astype(jnp.bfloat16)
    return paired.reshape(chips, count, width)


def chip_sums(paired):
    return lax.all_to_all(paired, "sc", split_axis=0, concat_axis=0, tiled=True)


def finish(back, weights):
    summed = jnp.sum(back.astype(jnp.float32), axis=0)
    return (summed * weights[:, None]).astype(jnp.bfloat16)


def shards(tokens, parents, expert_ids, route_weights, w_gate, w_up, w_down):
    count, width = tokens.shape
    picks_row = expert_ids.shape[1]
    experts = lax.axis_size("eg")
    group = lax.axis_index("eg")
    slots = 5 * count * picks_row // (4 * experts)
    nodes = jnp.arange(count, dtype=jnp.int32)
    parent_hot = (parents[:, None] == nodes[None, :]).astype(jnp.bfloat16)
    lifted = tokens.astype(jnp.float32) + jnp.dot(
        parent_hot, tokens, preferred_element_type=jnp.float32
    )
    normed = (lifted * lax.rsqrt(jnp.mean(lifted * lifted, axis=1, keepdims=True) + 1e-06)).astype(
        jnp.bfloat16
    )
    relative = (expert_ids - group) % experts
    picks = relative[:, :, None] == jnp.arange(experts, dtype=jnp.int32)[None, None, :]
    chosen = jnp.any(picks, axis=1).astype(jnp.int32)
    before = jnp.cumsum(chosen, axis=0) - chosen
    slot_iota = jnp.arange(slots, dtype=jnp.int32)
    place = (chosen[:, :, None] * (before[:, :, None] == slot_iota[None, None, :])) > 0
    weight_te = jnp.sum(jnp.where(picks, route_weights[:, :, None], 0.0), axis=1)
    packed = jnp.einsum(
        "tkc,td->kcd", place.astype(jnp.bfloat16), normed, preferred_element_type=jnp.float32
    ).astype(jnp.bfloat16)
    packed_w = jnp.sum(jnp.where(place, weight_te[:, :, None], 0.0), axis=0)
    weights = (w_gate[0], w_up[0], w_down[0])

    def shift(k):
        return [(g, (g + k) % experts) for g in range(experts)]

    away = [lax.ppermute(packed[k], "eg", shift(k)) for k in range(1, experts)]
    away_w = [lax.ppermute(packed_w[k], "eg", shift(k)) for k in range(1, experts)]
    own_rows = gather(packed[0])
    own_rows, away, away_w = lax.optimization_barrier((own_rows, away, away_w))
    own_parts = expert_parts(own_rows, *weights)
    away_rows = gather(jnp.concatenate(away, axis=0))
    own_parts, away_rows = lax.optimization_barrier((own_parts, away_rows))
    away_parts = expert_parts(away_rows, *weights)
    away_back = chip_sums(away_parts)
    done = finish(away_back, jnp.concatenate(away_w, axis=0))
    own_parts, done = lax.optimization_barrier((own_parts, done))
    own = finish(chip_sums(own_parts), packed_w[0])
    home = [own] + [
        lax.ppermute(done[(k - 1) * slots:k * slots], "eg", shift(experts - k))
        for k in range(1, experts)
    ]
    result = jnp.einsum(
        "tkc,kcd->td",
        place.astype(jnp.bfloat16),
        jnp.stack(home),
        preferred_element_type=jnp.float32,
    )
    return result.astype(jnp.bfloat16)


def solution(mesh):
    groups, ranks = mesh.devices.shape
    experts = ranks // SLICES
    cores = 2
    split = Mesh(
        mesh.devices.reshape(groups, experts, SLICES // cores, cores), ("grp", "eg", "sc", "core")
    )
    rows = ("grp", "eg", "sc", "core")
    placed = (
        P(rows, None),
        P(rows),
        P(rows, None),
        P(rows, None),
        P(("eg", "sc", "core"), None, None),
        P(("eg", "sc", "core"), None, None),
        P(("eg", "sc", "core"), None, None),
    )
    return jax.shard_map(
        shards, mesh=split, in_specs=placed, out_specs=P(rows, None), check_vma=False
    )
```

```python
import jax
import jax.numpy as jnp
from jax import lax
from jax.sharding import Mesh
from jax.sharding import PartitionSpec as P

SLICES = 8


def slice_hidden(rows, gate_up_w):
    both = jnp.dot(rows, gate_up_w, preferred_element_type=jnp.float32)
    gate, upper = jnp.split(both, 2, axis=1)
    return (jax.nn.silu(gate) * upper).astype(jnp.bfloat16)


def slice_down(hidden, down_w):
    return jnp.dot(hidden, down_w, preferred_element_type=jnp.float32).astype(jnp.bfloat16)


def gather(held):
    return lax.all_gather(held, ("core", "sc"), axis=0, tiled=True)


def expert_parts(gathered, gate_up_w, down_w):
    chips = lax.axis_size("sc")
    cores = lax.axis_size("core")
    count = gathered.shape[0] // (chips * cores)
    width = gathered.shape[1]
    hidden = slice_hidden(gathered, gate_up_w)
    halves = hidden.reshape(cores, chips * count, hidden.shape[1])
    core = lax.axis_index("core")
    swap = [(c, (c + 1) % cores) for c in range(cores)]
    sibling = lax.ppermute(slice_down(halves[(core + 1) % cores], down_w), "core", swap)
    kept = slice_down(halves[core], down_w)
    kept, sibling = lax.optimization_barrier((kept, sibling))
    paired = (kept.astype(jnp.float32) + sibling.astype(jnp.float32)).astype(jnp.bfloat16)
    return paired.reshape(chips, count, width)


def chip_sums(paired):
    return lax.all_to_all(paired, "sc", split_axis=0, concat_axis=0, tiled=True)


def finish(back, weights):
    summed = jnp.sum(back.astype(jnp.float32), axis=0)
    return (summed * weights[:, None]).astype(jnp.bfloat16)


def shards(tokens, parents, expert_ids, route_weights, w_gate, w_up, w_down):
    count, width = tokens.shape
    picks_row = expert_ids.shape[1]
    experts = lax.axis_size("eg")
    group = lax.axis_index("eg")
    slots = 5 * count * picks_row // (4 * experts)
    nodes = jnp.arange(count, dtype=jnp.int32)
    parent_hot = (parents[:, None] == nodes[None, :]).astype(jnp.bfloat16)
    lifted = tokens.astype(jnp.float32) + jnp.dot(
        parent_hot, tokens, preferred_element_type=jnp.float32
    )
    normed = (lifted * lax.rsqrt(jnp.mean(lifted * lifted, axis=1, keepdims=True) + 1e-06)).astype(
        jnp.bfloat16
    )
    relative = (expert_ids - group) % experts
    picks = relative[:, :, None] == jnp.arange(experts, dtype=jnp.int32)[None, None, :]
    chosen = jnp.any(picks, axis=1).astype(jnp.int32)
    before = jnp.cumsum(chosen, axis=0) - chosen
    slot_iota = jnp.arange(slots, dtype=jnp.int32)
    place = (chosen[:, :, None] * (before[:, :, None] == slot_iota[None, None, :])) > 0
    weight_te = jnp.sum(jnp.where(picks, route_weights[:, :, None], 0.0), axis=1)
    packed = jnp.einsum(
        "tkc,td->kcd", place.astype(jnp.bfloat16), normed, preferred_element_type=jnp.float32
    ).astype(jnp.bfloat16)
    packed_w = jnp.sum(jnp.where(place, weight_te[:, :, None], 0.0), axis=0)
    weights = (jnp.concatenate([w_gate[0], w_up[0]], axis=1), w_down[0])

    def shift(k):
        return [(g, (g + k) % experts) for g in range(experts)]

    away = [lax.ppermute(packed[k], "eg", shift(k)) for k in range(1, experts)]
    away_w = [lax.ppermute(packed_w[k], "eg", shift(k)) for k in range(1, experts)]
    own_rows = gather(packed[0])
    own_rows, away, away_w = lax.optimization_barrier((own_rows, away, away_w))
    own_parts = expert_parts(own_rows, *weights)
    away_rows = gather(jnp.concatenate(away, axis=0))
    own_parts, away_rows = lax.optimization_barrier((own_parts, away_rows))
    away_parts = expert_parts(away_rows, *weights)
    away_back = chip_sums(away_parts)
    done = finish(away_back, jnp.concatenate(away_w, axis=0))
    own_parts, done = lax.optimization_barrier((own_parts, done))
    own = finish(chip_sums(own_parts), packed_w[0])
    home = [own] + [
        lax.ppermute(done[(k - 1) * slots:k * slots], "eg", shift(experts - k))
        for k in range(1, experts)
    ]
    result = jnp.einsum(
        "tkc,kcd->td",
        place.astype(jnp.bfloat16),
        jnp.stack(home),
        preferred_element_type=jnp.float32,
    )
    return result.astype(jnp.bfloat16)


def solution(mesh):
    groups, ranks = mesh.devices.shape
    experts = ranks // SLICES
    cores = 2
    split = Mesh(
        mesh.devices.reshape(groups, experts, SLICES // cores, cores), ("grp", "eg", "sc", "core")
    )
    rows = ("grp", "eg", "sc", "core")
    placed = (
        P(rows, None),
        P(rows),
        P(rows, None),
        P(rows, None),
        P(("eg", "sc", "core"), None, None),
        P(("eg", "sc", "core"), None, None),
        P(("eg", "sc", "core"), None, None),
    )
    return jax.shard_map(
        shards, mesh=split, in_specs=placed, out_specs=P(rows, None), check_vma=False
    )
```

```python
import jax
import jax.numpy as jnp
from jax import lax
from jax.sharding import Mesh
from jax.sharding import PartitionSpec as P

SLICES = 8


def slice_hidden(rows, gate_up_w):
    both = jnp.dot(rows, gate_up_w, preferred_element_type=jnp.float32)
    gate, upper = jnp.split(both, 2, axis=1)
    return (jax.nn.silu(gate) * upper).astype(jnp.bfloat16)


def slice_down(hidden, down_w):
    return jnp.dot(hidden, down_w, preferred_element_type=jnp.float32).astype(jnp.bfloat16)


def gather(held):
    return lax.all_gather(held, ("core", "sc"), axis=0, tiled=True)


def expert_parts(gathered, gate_up_w, down_w):
    chips = lax.axis_size("sc")
    cores = lax.axis_size("core")
    count = gathered.shape[0] // (chips * cores)
    width = gathered.shape[1]
    halves = gathered.reshape(cores, chips * count, width)
    core = lax.axis_index("core")
    swap = [(c, (c + 1) % cores) for c in range(cores)]
    theirs = halves[(core + 1) % cores]
    sibling = lax.ppermute(slice_down(slice_hidden(theirs, gate_up_w), down_w), "core", swap)
    kept = slice_down(slice_hidden(halves[core], gate_up_w), down_w)
    kept, sibling = lax.optimization_barrier((kept, sibling))
    paired = (kept.astype(jnp.float32) + sibling.astype(jnp.float32)).astype(jnp.bfloat16)
    return paired.reshape(chips, count, width)


def chip_sums(paired):
    return lax.all_to_all(paired, "sc", split_axis=0, concat_axis=0, tiled=True)


def finish(back, weights):
    summed = jnp.sum(back.astype(jnp.float32), axis=0)
    return (summed * weights[:, None]).astype(jnp.bfloat16)


def shards(tokens, parents, expert_ids, route_weights, w_gate, w_up, w_down):
    count, width = tokens.shape
    picks_row = expert_ids.shape[1]
    experts = lax.axis_size("eg")
    group = lax.axis_index("eg")
    slots = 5 * count * picks_row // (4 * experts)
    nodes = jnp.arange(count, dtype=jnp.int32)
    parent_hot = (parents[:, None] == nodes[None, :]).astype(jnp.bfloat16)
    lifted = tokens.astype(jnp.float32) + jnp.dot(
        parent_hot, tokens, preferred_element_type=jnp.float32
    )
    normed = (lifted * lax.rsqrt(jnp.mean(lifted * lifted, axis=1, keepdims=True) + 1e-06)).astype(
        jnp.bfloat16
    )
    relative = (expert_ids - group) % experts
    picks = relative[:, :, None] == jnp.arange(experts, dtype=jnp.int32)[None, None, :]
    chosen = jnp.any(picks, axis=1).astype(jnp.int32)
    before = jnp.cumsum(chosen, axis=0) - chosen
    slot_iota = jnp.arange(slots, dtype=jnp.int32)
    place = (chosen[:, :, None] * (before[:, :, None] == slot_iota[None, None, :])) > 0
    weight_te = jnp.sum(jnp.where(picks, route_weights[:, :, None], 0.0), axis=1)
    packed = jnp.einsum(
        "tkc,td->kcd", place.astype(jnp.bfloat16), normed, preferred_element_type=jnp.float32
    ).astype(jnp.bfloat16)
    packed_w = jnp.sum(jnp.where(place, weight_te[:, :, None], 0.0), axis=0)
    weights = (jnp.concatenate([w_gate[0], w_up[0]], axis=1), w_down[0])

    def shift(k):
        return [(g, (g + k) % experts) for g in range(experts)]

    away = [lax.ppermute(packed[k], "eg", shift(k)) for k in range(1, experts)]
    away_w = [lax.ppermute(packed_w[k], "eg", shift(k)) for k in range(1, experts)]
    own_rows = gather(packed[0])
    own_rows, away, away_w = lax.optimization_barrier((own_rows, away, away_w))
    own_parts = expert_parts(own_rows, *weights)
    away_rows = gather(jnp.concatenate(away, axis=0))
    own_parts, away_rows = lax.optimization_barrier((own_parts, away_rows))
    away_parts = expert_parts(away_rows, *weights)
    away_back = chip_sums(away_parts)
    done = finish(away_back, jnp.concatenate(away_w, axis=0))
    own_parts, done = lax.optimization_barrier((own_parts, done))
    own = finish(chip_sums(own_parts), packed_w[0])
    home = [own] + [
        lax.ppermute(done[(k - 1) * slots:k * slots], "eg", shift(experts - k))
        for k in range(1, experts)
    ]
    result = jnp.einsum(
        "tkc,kcd->td",
        place.astype(jnp.bfloat16),
        jnp.stack(home),
        preferred_element_type=jnp.float32,
    )
    return result.astype(jnp.bfloat16)


def solution(mesh):
    groups, ranks = mesh.devices.shape
    experts = ranks // SLICES
    cores = 2
    split = Mesh(
        mesh.devices.reshape(groups, experts, SLICES // cores, cores), ("grp", "eg", "sc", "core")
    )
    rows = ("grp", "eg", "sc", "core")
    placed = (
        P(rows, None),
        P(rows),
        P(rows, None),
        P(rows, None),
        P(("eg", "sc", "core"), None, None),
        P(("eg", "sc", "core"), None, None),
        P(("eg", "sc", "core"), None, None),
    )
    return jax.shard_map(
        shards, mesh=split, in_specs=placed, out_specs=P(rows, None), check_vma=False
    )
```

```python
import jax
import jax.numpy as jnp
from jax import lax
from jax.sharding import Mesh
from jax.sharding import PartitionSpec as P

SLICES = 8


def slice_hidden(rows, gate_up_w):
    both = jnp.dot(rows, gate_up_w, preferred_element_type=jnp.float32)
    gate, upper = jnp.split(both, 2, axis=1)
    return (jax.nn.silu(gate) * upper).astype(jnp.bfloat16)


def slice_down(hidden, down_w):
    return jnp.dot(hidden, down_w, preferred_element_type=jnp.float32).astype(jnp.bfloat16)


def gather(held):
    return lax.all_gather(held, ("core", "sc"), axis=0, tiled=True)


def expert_parts(gathered, gate_up_w, down_w):
    chips = lax.axis_size("sc")
    cores = lax.axis_size("core")
    count = gathered.shape[0] // (chips * cores)
    width = gathered.shape[1]
    halves = gathered.reshape(cores, chips * count, width)
    core = lax.axis_index("core")
    swap = [(c, (c + 1) % cores) for c in range(cores)]
    theirs = halves[(core + 1) % cores]
    sibling = lax.ppermute(slice_down(slice_hidden(theirs, gate_up_w), down_w), "core", swap)
    kept = slice_down(slice_hidden(halves[core], gate_up_w), down_w)
    kept, sibling = lax.optimization_barrier((kept, sibling))
    paired = (kept.astype(jnp.float32) + sibling.astype(jnp.float32)).astype(jnp.bfloat16)
    return paired.reshape(chips, count, width)


def chip_sums(paired):
    return lax.all_to_all(paired, "sc", split_axis=0, concat_axis=0, tiled=True)


def finish(back, weights):
    summed = jnp.sum(back.astype(jnp.float32), axis=0)
    return (summed * weights[:, None]).astype(jnp.bfloat16)


def shards(tokens, parents, expert_ids, route_weights, w_gate, w_up, w_down):
    count, width = tokens.shape
    picks_row = expert_ids.shape[1]
    experts = lax.axis_size("eg")
    group = lax.axis_index("eg")
    slots = 5 * count * picks_row // (4 * experts)
    nodes = jnp.arange(count, dtype=jnp.int32)
    parent_hot = (parents[:, None] == nodes[None, :]).astype(jnp.bfloat16)
    lifted = tokens.astype(jnp.float32) + jnp.dot(
        parent_hot, tokens, preferred_element_type=jnp.float32
    )
    normed = (lifted * lax.rsqrt(jnp.mean(lifted * lifted, axis=1, keepdims=True) + 1e-06)).astype(
        jnp.bfloat16
    )
    relative = (expert_ids - group) % experts
    picks = relative[:, :, None] == jnp.arange(experts, dtype=jnp.int32)[None, None, :]
    chosen = jnp.any(picks, axis=1).astype(jnp.int32)
    before = jnp.cumsum(chosen, axis=0) - chosen
    slot_iota = jnp.arange(slots, dtype=jnp.int32)
    place = (chosen[:, :, None] * (before[:, :, None] == slot_iota[None, None, :])) > 0
    weight_te = jnp.sum(jnp.where(picks, route_weights[:, :, None], 0.0), axis=1)
    packed = jnp.einsum(
        "tkc,td->kcd", place.astype(jnp.bfloat16), normed, preferred_element_type=jnp.float32
    ).astype(jnp.bfloat16)
    packed_w = jnp.sum(jnp.where(place, weight_te[:, :, None], 0.0), axis=0)
    weights = (jnp.concatenate([w_gate[0], w_up[0]], axis=1), w_down[0])

    def shift(k):
        return [(g, (g + k) % experts) for g in range(experts)]

    away = [lax.ppermute(packed[k], "eg", shift(k)) for k in range(1, experts)]
    away_w = [lax.ppermute(packed_w[k], "eg", shift(k)) for k in range(1, experts)]
    own_rows = gather(packed[0])
    own_rows, away, away_w = lax.optimization_barrier((own_rows, away, away_w))
    own_parts = expert_parts(own_rows, *weights)
    away_rows = gather(jnp.concatenate(away, axis=0))
    own_parts, away_rows = lax.optimization_barrier((own_parts, away_rows))
    away_parts = expert_parts(away_rows, *weights)
    away_back = chip_sums(away_parts)
    done = finish(away_back, jnp.concatenate(away_w, axis=0))
    own_parts, done = lax.optimization_barrier((own_parts, done))
    own = finish(chip_sums(own_parts), packed_w[0])
    home = [own] + [
        lax.ppermute(done[(k - 1) * slots:k * slots], "eg", shift(experts - k))
        for k in range(1, experts)
    ]
    if picks_row == 1:
        spot = relative[:, 0] * slots + jnp.take_along_axis(before, relative, axis=1)[:, 0]
        return jnp.take(jnp.concatenate(home, axis=0), spot, axis=0, mode="clip")
    result = jnp.einsum(
        "tkc,kcd->td",
        place.astype(jnp.bfloat16),
        jnp.stack(home),
        preferred_element_type=jnp.float32,
    )
    return result.astype(jnp.bfloat16)


def solution(mesh):
    groups, ranks = mesh.devices.shape
    experts = ranks // SLICES
    cores = 2
    split = Mesh(
        mesh.devices.reshape(groups, experts, SLICES // cores, cores), ("grp", "eg", "sc", "core")
    )
    rows = ("grp", "eg", "sc", "core")
    placed = (
        P(rows, None),
        P(rows),
        P(rows, None),
        P(rows, None),
        P(("eg", "sc", "core"), None, None),
        P(("eg", "sc", "core"), None, None),
        P(("eg", "sc", "core"), None, None),
    )
    return jax.shard_map(
        shards, mesh=split, in_specs=placed, out_specs=P(rows, None), check_vma=False
    )
```

```python
import jax
import jax.numpy as jnp
from jax import lax
from jax.sharding import Mesh
from jax.sharding import PartitionSpec as P

SLICES = 8


def slice_hidden(rows, gate_up_w):
    gate_w, up_w = gate_up_w
    gate = jnp.dot(rows, gate_w, preferred_element_type=jnp.float32)
    upper = jnp.dot(rows, up_w, preferred_element_type=jnp.float32)
    return (jax.nn.silu(gate) * upper).astype(jnp.bfloat16)


def slice_down(hidden, down_w):
    return jnp.dot(hidden, down_w, preferred_element_type=jnp.float32).astype(jnp.bfloat16)


def gather(held):
    return lax.all_gather(held, ("core", "sc"), axis=0, tiled=True)


def expert_parts(gathered, gate_up_w, down_w):
    chips = lax.axis_size("sc")
    cores = lax.axis_size("core")
    count = gathered.shape[0] // (chips * cores)
    width = gathered.shape[1]
    halves = gathered.reshape(cores, chips * count, width)
    core = lax.axis_index("core")
    swap = [(c, (c + 1) % cores) for c in range(cores)]
    theirs = halves[(core + 1) % cores]
    sibling = lax.ppermute(slice_down(slice_hidden(theirs, gate_up_w), down_w), "core", swap)
    kept = slice_down(slice_hidden(halves[core], gate_up_w), down_w)
    kept, sibling = lax.optimization_barrier((kept, sibling))
    paired = (kept.astype(jnp.float32) + sibling.astype(jnp.float32)).astype(jnp.bfloat16)
    return paired.reshape(chips, count, width)


def chip_sums(paired):
    return lax.all_to_all(paired, "sc", split_axis=0, concat_axis=0, tiled=True)


def finish(back, weights):
    summed = jnp.sum(back.astype(jnp.float32), axis=0)
    return (summed * weights[:, None]).astype(jnp.bfloat16)


def shards(tokens, parents, expert_ids, route_weights, w_gate, w_up, w_down):
    count, width = tokens.shape
    picks_row = expert_ids.shape[1]
    experts = lax.axis_size("eg")
    group = lax.axis_index("eg")
    slots = 5 * count * picks_row // (4 * experts)
    nodes = jnp.arange(count, dtype=jnp.int32)
    parent_hot = (parents[:, None] == nodes[None, :]).astype(jnp.bfloat16)
    lifted = tokens.astype(jnp.float32) + jnp.dot(
        parent_hot, tokens, preferred_element_type=jnp.float32
    )
    normed = (lifted * lax.rsqrt(jnp.mean(lifted * lifted, axis=1, keepdims=True) + 1e-06)).astype(
        jnp.bfloat16
    )
    relative = (expert_ids - group) % experts
    picks = relative[:, :, None] == jnp.arange(experts, dtype=jnp.int32)[None, None, :]
    chosen = jnp.any(picks, axis=1).astype(jnp.int32)
    before = jnp.cumsum(chosen, axis=0) - chosen
    slot_iota = jnp.arange(slots, dtype=jnp.int32)
    place = (chosen[:, :, None] * (before[:, :, None] == slot_iota[None, None, :])) > 0
    weight_te = jnp.sum(jnp.where(picks, route_weights[:, :, None], 0.0), axis=1)
    packed = jnp.einsum(
        "tkc,td->kcd", place.astype(jnp.bfloat16), normed, preferred_element_type=jnp.float32
    ).astype(jnp.bfloat16)
    packed_w = jnp.sum(jnp.where(place, weight_te[:, :, None], 0.0), axis=0)
    weights = ((w_gate[0], w_up[0]), w_down[0])

    def shift(k):
        return [(g, (g + k) % experts) for g in range(experts)]

    away = [lax.ppermute(packed[k], "eg", shift(k)) for k in range(1, experts)]
    away_w = [lax.ppermute(packed_w[k], "eg", shift(k)) for k in range(1, experts)]
    own_rows = gather(packed[0])
    own_rows, away, away_w = lax.optimization_barrier((own_rows, away, away_w))
    own_parts = expert_parts(own_rows, *weights)
    away_rows = gather(jnp.concatenate(away, axis=0))
    own_parts, away_rows = lax.optimization_barrier((own_parts, away_rows))
    away_parts = expert_parts(away_rows, *weights)
    away_back = chip_sums(away_parts)
    done = finish(away_back, jnp.concatenate(away_w, axis=0))
    own_parts, done = lax.optimization_barrier((own_parts, done))
    own = finish(chip_sums(own_parts), packed_w[0])
    home = [own] + [
        lax.ppermute(done[(k - 1) * slots:k * slots], "eg", shift(experts - k))
        for k in range(1, experts)
    ]
    result = jnp.einsum(
        "tkc,kcd->td",
        place.astype(jnp.bfloat16),
        jnp.stack(home),
        preferred_element_type=jnp.float32,
    )
    return result.astype(jnp.bfloat16)


def solution(mesh):
    groups, ranks = mesh.devices.shape
    experts = ranks // SLICES
    cores = 2
    split = Mesh(
        mesh.devices.reshape(groups, experts, SLICES // cores, cores), ("grp", "eg", "sc", "core")
    )
    rows = ("grp", "eg", "sc", "core")
    placed = (
        P(rows, None),
        P(rows),
        P(rows, None),
        P(rows, None),
        P(("eg", "sc", "core"), None, None),
        P(("eg", "sc", "core"), None, None),
        P(("eg", "sc", "core"), None, None),
    )
    return jax.shard_map(
        shards, mesh=split, in_specs=placed, out_specs=P(rows, None), check_vma=False
    )
```
